256 devices in a mesh: section: 16 (over y, x), dp: 16 (over z, core).
Axes of the slice: x: 4, y: 4, z: 8, core: 2. Of those that a mesh axis runs over, the one named last changes fastest.
Arguments:
- hidden: bfloat16 [16, 256, 8192], P('dp', 'section'), may hold values from -1500 to 1500
- head: bfloat16 [65536, 8192], P('section', 'dp'), may hold values from -0.0625 to 0.0625
- block_id: int32 [16, 16], P(None, 'section'), may hold values from 0 to 7
- block_live: int32 [16, 16], P(None, 'section'), may hold values from 0 to 1, as said below
- teacher: bfloat16 [16, 256, 8192], P('dp', None, 'section'), may hold values from -400 to 400
Outputs:
- grad_hidden: bfloat16 [16, 256, 8192], P('dp', 'section')
- grad_head: bfloat16 [65536, 8192], P('section', 'dp')
The draws below stay inside these ranges and needn't reach their ends.
Inputs may be any that keep to these rules, and one draw needn't show every extreme that they name: `block_live`: every micro-batch has at least one live section.
All inputs are finite; a program needn't handle non-finite values.
Results may differ from the reference program's by a relative error of at most 0.0056.
Values may be sent and summed in bfloat16 or wider, within the bound.
No kernel may reach another device: no remote copies, remote signals or barrier semaphores. Data moves between devices by JAX's collectives and lax.ppermute only.
A program may use at most 128 MiB of HBM per device.

```python
import jax
import jax.numpy as jnp
from jax import lax

D = 8192
VB = 512
BLK_DEV = 8
TOK = 256
MBS = 16
V = 65536
N_SECTION = 16


def draw_hidden(key, part):
    base = jax.random.normal(jax.random.fold_in(key, 11), (MBS, TOK, D), jnp.float32)
    return base.astype(jnp.bfloat16)


def draw_teacher(key, part):
    base = 3.0 * jax.random.normal(jax.random.fold_in(key, 21), (MBS, TOK, N_SECTION * VB), jnp.float32)
    return base.astype(jnp.bfloat16)


def draw_block_live(key, part):
    rolls = jax.random.randint(jax.random.fold_in(key, 31), (MBS, N_SECTION), 0, 10)
    section_pos = jnp.arange(N_SECTION, dtype=jnp.int32)[None, :]
    batch_pos = jnp.arange(MBS, dtype=jnp.int32)[:, None]
    forced = section_pos == batch_pos % N_SECTION
    return ((rolls < 7) | forced).astype(jnp.int32)


def place_ends(entries, key, least, largest):
    longest = entries.shape.index(max(entries.shape))
    spots = []
    for shift in (0, 1):
        where = [jax.random.randint(jax.random.fold_in(key, axis), (), 0, length) for axis, length in enumerate(entries.shape)]
        where[longest] = (where[longest] + shift) % entries.shape[longest]
        spots.append(tuple(where))
    return entries.at[spots[0]].set(least).at[spots[1]].set(largest)


def level_of(rng, dims, split, smallest, largest):
    level, own = 1.0, jax.random.fold_in(rng, 6)
    for axis_at, blocks in split:
        draws = jnp.exp(jax.random.uniform(jax.random.fold_in(own, axis_at), (blocks,), jnp.float32, smallest / len(split), largest / len(split)))
        level = level * jnp.repeat(draws, dims[axis_at] // blocks).reshape([-1 if axis == axis_at else 1 for axis in range(len(dims))])
    return level


def bell_draw(stream_key, shape, deviation, most, pieces=(), kind=jnp.bfloat16):
    entries = jax.random.normal(stream_key, shape, jnp.float32) * deviation
    if len(pieces) > 0:
        entries = level_of(stream_key, shape, pieces, -0.22, 0.18) * entries
    return jnp.clip(entries, min=-most, max=most).astype(kind)


def setup_inputs(seed: int = 0) -> dict:
    seeds = jax.random.split(jax.random.key(seed), 6)
    return {
        "hidden": draw_hidden(jax.random.fold_in(seeds[5], 71), 0),
        "head": bell_draw(seeds[1], (V, D), D ** -0.5, 0.0625, ((0, 16), (1, 16))),
        "block_id": place_ends(jax.random.randint(seeds[2], (MBS, N_SECTION), 0, BLK_DEV), jax.random.fold_in(seeds[2], 1), 0, BLK_DEV - 1).astype(jnp.int32),
        "block_live": draw_block_live(jax.random.fold_in(seeds[5], 71), 0),
        "teacher": draw_teacher(jax.random.fold_in(seeds[5], 71), 0),
    }


neg_fill = -1.0e30


def reference(hidden, head, block_id, block_live, teacher):
    table = head.reshape(N_SECTION * BLK_DEV, VB, D)
    offsets = (jnp.arange(N_SECTION, dtype=jnp.int32) * BLK_DEV)[None, :]
    chosen = (block_id + offsets).astype(jnp.int32)
    counts = jnp.sum(block_live, axis=1).astype(jnp.float32)

    def forward(item):
        rows_hidden, picks, flags, scores, total = item
        rows = table[picks].astype(jnp.float32)
        logits = jnp.einsum("td,srd->tsr", rows_hidden.astype(jnp.float32), rows)
        mask = (flags > 0)[None, :, None]
        teach = scores.reshape(TOK, N_SECTION, VB).astype(jnp.float32)

        def probs(values):
            masked = jnp.where(mask, values, neg_fill)
            top = jnp.max(masked, axis=(1, 2), keepdims=True)
            expo = jnp.where(mask, jnp.exp(values - top), 0.0)
            return expo / jnp.sum(expo, axis=(1, 2), keepdims=True)

        grad = (VB * total * (probs(logits) - probs(teach))).astype(jnp.bfloat16)
        ghid = jnp.einsum("tsr,srd->td", grad.astype(jnp.float32), rows).astype(jnp.bfloat16)
        return grad, ghid

    logit_grad, grad_hidden = lax.map(forward, (hidden, chosen, block_live, teacher, counts))

    def per_section(section):
        grads = lax.dynamic_index_in_dim(logit_grad, section, 2, keepdims=False)
        contrib = jnp.einsum("mtr,mtd->mrd", grads.astype(jnp.float32), hidden.astype(jnp.float32)).astype(jnp.bfloat16)
        ids = lax.dynamic_index_in_dim(block_id, section, 1, keepdims=False)
        flags = lax.dynamic_index_in_dim(block_live, section, 1, keepdims=False)
        select = jnp.where((flags[:, None] > 0) & (ids[:, None] == jnp.arange(BLK_DEV, dtype=jnp.int32)[None, :]), 1.0, 0.0).astype(jnp.float32)
        return jnp.einsum("mb,mrd->brd", select, contrib.astype(jnp.float32)).astype(jnp.bfloat16)

    grad_head = lax.map(per_section, jnp.arange(N_SECTION, dtype=jnp.int32)).reshape(V, D)
    return grad_hidden, grad_head
```

```python
import jax
import jax.numpy as jnp
from jax import lax
from jax.sharding import PartitionSpec as P

neg_fill = -1e30


def local(hidden, head, block_id, block_live, teacher):
    my_replica = lax.axis_index("dp")
    n_dp = lax.axis_size("dp")
    tok_local = hidden.shape[1]
    model_width = hidden.shape[2]
    block_rows = teacher.shape[2]
    col_width = head.shape[1]
    blocks = head.shape[0] // block_rows
    table = head.reshape(blocks, block_rows, col_width)
    block_ids = block_id[:, 0]
    live_flags = block_live[:, 0]
    n_mb = block_ids.shape[0]

    pieces = hidden.reshape(1, tok_local, n_dp, col_width)
    pieces = lax.all_to_all(pieces, "dp", split_axis=2, concat_axis=0, tiled=True)
    hid_w = lax.all_gather(pieces, "section", axis=1, tiled=True).reshape(n_mb, -1, col_width)

    picked = jnp.take(table, block_ids, axis=0)
    part = jnp.einsum("mtw,mrw->mtr", hid_w, picked, preferred_element_type=jnp.float32)
    logits = lax.psum_scatter(part, "dp", scatter_dimension=0, tiled=True)[0]

    own_live = lax.dynamic_index_in_dim(live_flags, my_replica, 0, keepdims=False) > 0
    teach = teacher[0].astype(jnp.float32)
    live_value = jnp.where(own_live, 1.0, 0.0).astype(jnp.float32)
    stud_local = jnp.where(own_live, jnp.max(logits, axis=1), neg_fill)
    teach_local = jnp.where(own_live, jnp.max(teach, axis=1), neg_fill)
    stud_top, teach_top = lax.pmax((stud_local, teach_local), "section")
    stud_part = jnp.where(own_live, jnp.sum(jnp.exp(logits - stud_top[:, None]), axis=1), 0.0)
    teach_part = jnp.where(own_live, jnp.sum(jnp.exp(teach - teach_top[:, None]), axis=1), 0.0)
    stud_total, teach_total, live_count = lax.psum((stud_part, teach_part, live_value), "section")
    student = jnp.where(own_live, jnp.exp(logits - stud_top[:, None]) / stud_total[:, None], 0.0)
    teach_prob = jnp.where(
        own_live, jnp.exp(teach - teach_top[:, None]) / teach_total[:, None], 0.0
    )
    logit_grad = (block_rows * live_count * (student - teach_prob)).astype(jnp.bfloat16)
    grads = lax.all_gather(logit_grad[None], "dp", axis=0, tiled=True)

    contrib = jnp.einsum(
        "mtr,mtw->mrw", grads, hid_w, preferred_element_type=jnp.float32
    ).astype(jnp.bfloat16)
    block_range = jnp.arange(blocks, dtype=jnp.int32)[None, :]
    selector = jnp.where(
        (live_flags[:, None] > 0) & (block_ids[:, None] == block_range), 1.0, 0.0
    ).astype(jnp.bfloat16)
    grad_head = jnp.einsum("mb,mrw->brw", selector, contrib, preferred_element_type=jnp.float32)
    grad_head = grad_head.astype(jnp.bfloat16).reshape(blocks * block_rows, col_width)

    ghid = jnp.einsum("mtr,mrw->mtw", grads, picked, preferred_element_type=jnp.float32)
    ghid = lax.psum_scatter(ghid, "section", scatter_dimension=1, tiled=True).astype(jnp.bfloat16)
    ghid = lax.all_to_all(ghid, "dp", split_axis=0, concat_axis=2, tiled=True)
    grad_hidden = ghid.reshape(1, tok_local, model_width)
    return (grad_hidden, grad_head)


def solution(mesh):
    placed = (
        P("dp", "section", None),
        P("section", "dp"),
        P(None, "section"),
        P(None, "section"),
        P("dp", None, "section"),
    )
    return jax.shard_map(
        local,
        mesh=mesh,
        in_specs=placed,
        out_specs=(P("dp", "section", None), P("section", "dp")),
        check_vma=False,
    )
```

```python
import jax
import jax.numpy as jnp
from jax import lax
from jax.sharding import PartitionSpec as P

neg_fill = -1e30


def local(hidden, head, block_id, block_live, teacher):
    my_replica = lax.axis_index("dp")
    n_dp = lax.axis_size("dp")
    tok_local = hidden.shape[1]
    model_width = hidden.shape[2]
    block_rows = teacher.shape[2]
    col_width = head.shape[1]
    blocks = head.shape[0] // block_rows
    table = head.reshape(blocks, block_rows, col_width)
    block_ids = block_id[:, 0]
    live_flags = block_live[:, 0]
    n_mb = block_ids.shape[0]

    pieces = hidden.reshape(1, tok_local, n_dp, col_width)
    pieces = lax.all_to_all(pieces, "dp", split_axis=2, concat_axis=0, tiled=True)
    hid_w = lax.all_gather(pieces, "section", axis=1, tiled=True).reshape(n_mb, -1, col_width)

    picked = jnp.take(table, block_ids, axis=0)
    part = jnp.einsum("mtw,mrw->mtr", hid_w, picked, preferred_element_type=jnp.float32)
    logits = lax.psum_scatter(part, "dp", scatter_dimension=0, tiled=True)[0]

    own_live = lax.dynamic_index_in_dim(live_flags, my_replica, 0, keepdims=False) > 0
    teach = teacher[0].astype(jnp.float32)
    live_value = jnp.where(own_live, 1.0, 0.0).astype(jnp.float32)

    def local_stats(values):
        top = jnp.where(own_live, jnp.max(values, axis=1), neg_fill)
        total = jnp.where(own_live, jnp.sum(jnp.exp(values - top[:, None]), axis=1), 0.0)
        return top, total

    def merged(tops, totals):
        top = jnp.max(tops, axis=0)
        return top, jnp.sum(totals * jnp.exp(tops - top[None, :]), axis=0)

    teach_top_s, teach_sum_s = local_stats(teach)
    live_row = jnp.broadcast_to(live_value, teach_top_s.shape)
    teach_all = lax.all_gather(jnp.stack([teach_top_s, teach_sum_s, live_row]), "section")
    teach_top, teach_total = merged(teach_all[:, 0], teach_all[:, 1])
    live_count = jnp.sum(teach_all[:, 2, 0])

    stud_top_s, stud_sum_s = local_stats(logits)
    stud_all = lax.all_gather(jnp.stack([stud_top_s, stud_sum_s]), "section")
    stud_top, stud_total = merged(stud_all[:, 0], stud_all[:, 1])

    student = jnp.where(own_live, jnp.exp(logits - stud_top[:, None]) / stud_total[:, None], 0.0)
    teach_prob = jnp.where(
        own_live, jnp.exp(teach - teach_top[:, None]) / teach_total[:, None], 0.0
    )
    logit_grad = (block_rows * live_count * (student - teach_prob)).astype(jnp.bfloat16)
    grads = lax.all_gather(logit_grad[None], "dp", axis=0, tiled=True)

    contrib = jnp.einsum(
        "mtr,mtw->mrw", grads, hid_w, preferred_element_type=jnp.float32
    ).astype(jnp.bfloat16)
    block_range = jnp.arange(blocks, dtype=jnp.int32)[None, :]
    selector = jnp.where(
        (live_flags[:, None] > 0) & (block_ids[:, None] == block_range), 1.0, 0.0
    ).astype(jnp.bfloat16)
    grad_head = jnp.einsum("mb,mrw->brw", selector, contrib, preferred_element_type=jnp.float32)
    grad_head = grad_head.astype(jnp.bfloat16).reshape(blocks * block_rows, col_width)

    ghid = jnp.einsum("mtr,mrw->mtw", grads, picked, preferred_element_type=jnp.float32)
    ghid = lax.psum_scatter(ghid, "section", scatter_dimension=1, tiled=True).astype(jnp.bfloat16)
    ghid = lax.all_to_all(ghid, "dp", split_axis=0, concat_axis=2, tiled=True)
    grad_hidden = ghid.reshape(1, tok_local, model_width)
    return (grad_hidden, grad_head)


def solution(mesh):
    placed = (
        P("dp", "section", None),
        P("section", "dp"),
        P(None, "section"),
        P(None, "section"),
        P("dp", None, "section"),
    )
    return jax.shard_map(
        local,
        mesh=mesh,
        in_specs=placed,
        out_specs=(P("dp", "section", None), P("section", "dp")),
        check_vma=False,
    )
```

```python
import jax
import jax.numpy as jnp
from jax import lax
from jax.sharding import Mesh, PartitionSpec as P

neg_fill = -1e30


def local(hidden, head, block_id, block_live, teacher):
    z_at = lax.axis_index("z")
    core_at = lax.axis_index("core")
    n_z = lax.axis_size("z")
    n_core = lax.axis_size("core")
    my_replica = z_at * n_core + core_at
    odd = core_at == 1
    tok_local = hidden.shape[1]
    model_width = hidden.shape[2]
    block_rows = teacher.shape[2]
    col_width = head.shape[1]
    blocks = head.shape[0] // block_rows
    table = head.reshape(blocks, block_rows, col_width)
    block_ids = block_id[:, 0]
    live_flags = block_live[:, 0]
    swap = [(0, 1), (1, 0)]

    ids_by = block_ids.reshape(n_z, n_core)
    own_ids = lax.dynamic_index_in_dim(ids_by, core_at, 1, keepdims=False)
    sib_ids = lax.dynamic_index_in_dim(ids_by, 1 - core_at, 1, keepdims=False)

    pieces = hidden[0].reshape(tok_local, n_z, n_core, col_width)
    pieces = jnp.where(odd, pieces[:, :, ::-1, :], pieces)
    pieces = pieces.reshape(1, tok_local, n_z, n_core * col_width)
    pieces = lax.all_to_all(pieces, "z", split_axis=2, concat_axis=0, tiled=True)
    hid_w = lax.all_gather(pieces, "section", axis=1, tiled=True).reshape(n_z, -1, n_core * col_width)
    hid_own = hid_w[:, :, :col_width]
    hid_sib = hid_w[:, :, col_width:]

    own_rows = jnp.take(table, own_ids, axis=0)
    sib_rows = lax.ppermute(jnp.take(table, sib_ids, axis=0), "core", swap)

    own_live = lax.dynamic_index_in_dim(live_flags, my_replica, 0, keepdims=False) > 0
    teach = teacher[0].astype(jnp.float32)
    live_value = jnp.where(own_live, 1.0, 0.0).astype(jnp.float32)

    def local_stats(values):
        top = jnp.where(own_live, jnp.max(values, axis=1), neg_fill)
        total = jnp.where(own_live, jnp.sum(jnp.exp(values - top[:, None]), axis=1), 0.0)
        return top, total

    def merged(tops, totals):
        top = jnp.max(tops, axis=0)
        return top, jnp.sum(totals * jnp.exp(tops - top[None, :]), axis=0)

    teach_top_s, teach_sum_s = local_stats(teach)
    live_row = jnp.broadcast_to(live_value, teach_top_s.shape)
    teach_all = lax.all_gather(jnp.stack([teach_top_s, teach_sum_s, live_row]), "section")
    teach_all, hid_own, hid_sib = lax.optimization_barrier((teach_all, hid_own, hid_sib))
    teach_top, teach_total = merged(teach_all[:, 0], teach_all[:, 1])
    live_count = jnp.sum(teach_all[:, 2, 0])

    part = jnp.einsum("mtw,mrw->mtr", hid_own, own_rows, preferred_element_type=jnp.float32)
    part = part + jnp.einsum("mtw,mrw->mtr", hid_sib, sib_rows, preferred_element_type=jnp.float32)
    logits = lax.psum_scatter(part, "z", scatter_dimension=0, tiled=True)[0]

    stud_top_s, stud_sum_s = local_stats(logits)
    stud_all = lax.all_gather(jnp.stack([stud_top_s, stud_sum_s]), "section")
    stud_top, stud_total = merged(stud_all[:, 0], stud_all[:, 1])

    student = jnp.where(own_live, jnp.exp(logits - stud_top[:, None]) / stud_total[:, None], 0.0)
    teach_prob = jnp.where(
        own_live, jnp.exp(teach - teach_top[:, None]) / teach_total[:, None], 0.0
    )
    logit_grad = (block_rows * live_count * (student - teach_prob)).astype(jnp.bfloat16)
    grads = lax.all_gather(logit_grad[None], "z", axis=0, tiled=True)

    ghid = jnp.concatenate(
        [
            jnp.einsum("mtr,mrw->mtw", grads, own_rows, preferred_element_type=jnp.float32),
            jnp.einsum("mtr,mrw->mtw", grads, sib_rows, preferred_element_type=jnp.float32),
        ],
        axis=2,
    )
    ghid = lax.psum_scatter(ghid, "section", scatter_dimension=1, tiled=True).astype(jnp.bfloat16)
    ghid = lax.all_to_all(ghid[:, :, None], "z", split_axis=0, concat_axis=2, tiled=True)
    ghid = ghid.reshape(tok_local, n_z, n_core, col_width)
    ghid = jnp.where(odd, ghid[:, :, ::-1, :], ghid)
    grad_hidden = ghid.reshape(1, tok_local, model_width)

    contrib_own = jnp.einsum(
        "mtr,mtw->mrw", grads, hid_own, preferred_element_type=jnp.float32
    ).astype(jnp.bfloat16)
    contrib_sib = jnp.einsum(
        "mtr,mtw->mrw", grads, hid_sib, preferred_element_type=jnp.float32
    ).astype(jnp.bfloat16)
    contrib_got = lax.ppermute(contrib_sib, "core", swap)
    block_range = jnp.arange(blocks, dtype=jnp.int32)[None, :]
    selector = jnp.where(
        (live_flags[:, None] > 0) & (block_ids[:, None] == block_range), 1.0, 0.0
    ).astype(jnp.bfloat16)
    sel_by = selector.reshape(n_z, n_core, blocks)
    sel_own = lax.dynamic_index_in_dim(sel_by, core_at, 1, keepdims=False)
    sel_sib = lax.dynamic_index_in_dim(sel_by, 1 - core_at, 1, keepdims=False)
    grad_head = jnp.einsum("mb,mrw->brw", sel_own, contrib_own, preferred_element_type=jnp.float32)
    grad_head = grad_head + jnp.einsum(
        "mb,mrw->brw", sel_sib, contrib_got, preferred_element_type=jnp.float32
    )
    grad_head = grad_head.astype(jnp.bfloat16).reshape(blocks * block_rows, col_width)
    return (grad_hidden, grad_head)


def solution(mesh):
    n_section, n_dp = mesh.devices.shape
    chips = Mesh(mesh.devices.reshape(n_section, n_dp // 2, 2), ("section", "z", "core"))
    dp = ("z", "core")
    placed = (
        P(dp, "section", None),
        P("section", dp),
        P(None, "section"),
        P(None, "section"),
        P(dp, None, "section"),
    )
    return jax.shard_map(
        local,
        mesh=chips,
        in_specs=placed,
        out_specs=(P(dp, "section", None), P("section", dp)),
        check_vma=False,
    )
```

```python
import jax
import jax.numpy as jnp
from jax import lax
from jax.sharding import Mesh, PartitionSpec as P

neg_fill = -1e30


def local(hidden, head, block_id, block_live, teacher):
    z_at = lax.axis_index("z")
    core_at = lax.axis_index("core")
    n_z = lax.axis_size("z")
    n_core = lax.axis_size("core")
    my_replica = z_at * n_core + core_at
    odd = core_at == 1
    tok_local = hidden.shape[1]
    model_width = hidden.shape[2]
    block_rows = teacher.shape[2]
    col_width = head.shape[1]
    blocks = head.shape[0] // block_rows
    table = head.reshape(blocks, block_rows, col_width)
    block_ids = block_id[:, 0]
    live_flags = block_live[:, 0]
    swap = [(0, 1), (1, 0)]

    ids_by = block_ids.reshape(n_z, n_core)
    own_ids = lax.dynamic_index_in_dim(ids_by, core_at, 1, keepdims=False)
    sib_ids = lax.dynamic_index_in_dim(ids_by, 1 - core_at, 1, keepdims=False)

    pieces = hidden[0].reshape(tok_local, n_z, n_core, col_width)
    pieces = jnp.where(odd, pieces[:, :, ::-1, :], pieces)
    pieces = pieces.reshape(1, tok_local, n_z, n_core * col_width)
    pieces = lax.all_to_all(pieces, "z", split_axis=2, concat_axis=0, tiled=True)
    hid_w = lax.all_gather(pieces, "section", axis=1, tiled=True).reshape(n_z, -1, n_core * col_width)

    own_rows = jnp.take(table, own_ids, axis=0)
    sib_rows = lax.ppermute(jnp.take(table, sib_ids, axis=0), "core", swap)
    rows = jnp.concatenate([own_rows, sib_rows], axis=2)

    own_live = lax.dynamic_index_in_dim(live_flags, my_replica, 0, keepdims=False) > 0
    teach = teacher[0].astype(jnp.float32)
    live_value = jnp.where(own_live, 1.0, 0.0).astype(jnp.float32)

    def local_stats(values):
        top = jnp.where(own_live, jnp.max(values, axis=1), neg_fill)
        total = jnp.where(own_live, jnp.sum(jnp.exp(values - top[:, None]), axis=1), 0.0)
        return top, total

    def merged(tops, totals):
        top = jnp.max(tops, axis=0)
        return top, jnp.sum(totals * jnp.exp(tops - top[None, :]), axis=0)

    teach_top_s, teach_sum_s = local_stats(teach)
    live_row = jnp.broadcast_to(live_value, teach_top_s.shape)
    teach_all = lax.all_gather(jnp.stack([teach_top_s, teach_sum_s, live_row]), "section")
    teach_all, hid_w = lax.optimization_barrier((teach_all, hid_w))
    teach_top, teach_total = merged(teach_all[:, 0], teach_all[:, 1])
    live_count = jnp.sum(teach_all[:, 2, 0])

    part = jnp.einsum("mtw,mrw->mtr", hid_w, rows, preferred_element_type=jnp.float32)
    logits = lax.psum_scatter(part, "z", scatter_dimension=0, tiled=True)[0]

    stud_top_s, stud_sum_s = local_stats(logits)
    stud_all = lax.all_gather(jnp.stack([stud_top_s, stud_sum_s]), "section")
    stud_top, stud_total = merged(stud_all[:, 0], stud_all[:, 1])

    student = jnp.where(own_live, jnp.exp(logits - stud_top[:, None]) / stud_total[:, None], 0.0)
    teach_prob = jnp.where(
        own_live, jnp.exp(teach - teach_top[:, None]) / teach_total[:, None], 0.0
    )
    logit_grad = (block_rows * live_count * (student - teach_prob)).astype(jnp.bfloat16)
    grads = lax.all_gather(logit_grad[None], "z", axis=0, tiled=True)

    contrib_sib = jnp.einsum(
        "mtr,mtw->mrw", grads, hid_w[:, :, col_width:], preferred_element_type=jnp.float32
    ).astype(jnp.bfloat16)
    contrib_got = lax.ppermute(contrib_sib, "core", swap)
    contrib_own = jnp.einsum(
        "mtr,mtw->mrw", grads, hid_w[:, :, :col_width], preferred_element_type=jnp.float32
    ).astype(jnp.bfloat16)

    ghid = jnp.einsum("mtr,mrw->mtw", grads, rows, preferred_element_type=jnp.float32)
    ghid, contrib_got = lax.optimization_barrier((ghid, contrib_got))
    ghid = lax.psum_scatter(ghid, "section", scatter_dimension=1, tiled=True).astype(jnp.bfloat16)
    ghid = lax.all_to_all(ghid[:, :, None], "z", split_axis=0, concat_axis=2, tiled=True)
    ghid = ghid.reshape(tok_local, n_z, n_core, col_width)
    ghid = jnp.where(odd, ghid[:, :, ::-1, :], ghid)
    grad_hidden = ghid.reshape(1, tok_local, model_width)

    block_range = jnp.arange(blocks, dtype=jnp.int32)[None, :]
    selector = jnp.where(
        (live_flags[:, None] > 0) & (block_ids[:, None] == block_range), 1.0, 0.0
    ).astype(jnp.bfloat16)
    sel_by = selector.reshape(n_z, n_core, blocks)
    sel_own = lax.dynamic_index_in_dim(sel_by, core_at, 1, keepdims=False)
    sel_sib = lax.dynamic_index_in_dim(sel_by, 1 - core_at, 1, keepdims=False)
    grad_head = jnp.einsum("mb,mrw->brw", sel_own, contrib_own, preferred_element_type=jnp.float32)
    grad_head = grad_head + jnp.einsum(
        "mb,mrw->brw", sel_sib, contrib_got, preferred_element_type=jnp.float32
    )
    grad_head = grad_head.astype(jnp.bfloat16).reshape(blocks * block_rows, col_width)
    return (grad_hidden, grad_head)


def solution(mesh):
    n_section, n_dp = mesh.devices.shape
    chips = Mesh(mesh.devices.reshape(n_section, n_dp // 2, 2), ("section", "z", "core"))
    dp = ("z", "core")
    placed = (
        P(dp, "section", None),
        P("section", dp),
        P(None, "section"),
        P(None, "section"),
        P(dp, None, "section"),
    )
    return jax.shard_map(
        local,
        mesh=chips,
        in_specs=placed,
        out_specs=(P(dp, "section", None), P("section", dp)),
        check_vma=False,
    )
```

```python
import jax
import jax.numpy as jnp
from jax import lax
from jax.sharding import Mesh, PartitionSpec as P

neg_fill = -1e30


def local(hidden, head, block_id, block_live, teacher):
    z_at = lax.axis_index("z")
    core_at = lax.axis_index("core")
    n_z = lax.axis_size("z")
    n_core = lax.axis_size("core")
    my_replica = z_at * n_core + core_at
    odd = core_at == 1
    tok_local = hidden.shape[1]
    model_width = hidden.shape[2]
    block_rows = teacher.shape[2]
    col_width = head.shape[1]
    blocks = head.shape[0] // block_rows
    table = head.reshape(blocks, block_rows, col_width)
    block_ids = block_id[:, 0]
    live_flags = block_live[:, 0]
    swap = [(0, 1), (1, 0)]

    ids_by = block_ids.reshape(n_z, n_core)
    own_ids = lax.dynamic_index_in_dim(ids_by, core_at, 1, keepdims=False)
    sib_ids = lax.dynamic_index_in_dim(ids_by, 1 - core_at, 1, keepdims=False)

    pieces = hidden[0].reshape(tok_local, n_z, n_core, col_width)
    pieces = jnp.where(odd, pieces[:, :, ::-1, :], pieces)
    pieces = pieces.reshape(1, tok_local, n_z, n_core * col_width)
    pieces = lax.all_to_all(pieces, "z", split_axis=2, concat_axis=0, tiled=True)
    hid_w = lax.all_gather(pieces, "section", axis=1, tiled=True).reshape(n_z, -1, n_core * col_width)

    own_rows = jnp.take(table, own_ids, axis=0)
    sib_rows = lax.ppermute(jnp.take(table, sib_ids, axis=0), "core", swap)
    rows = jnp.concatenate([own_rows, sib_rows], axis=2)

    own_live = lax.dynamic_index_in_dim(live_flags, my_replica, 0, keepdims=False) > 0
    teach = teacher[0].astype(jnp.float32)
    live_value = jnp.where(own_live, 1.0, 0.0).astype(jnp.float32)

    def local_stats(values):
        top = jnp.where(own_live, jnp.max(values, axis=1), neg_fill)
        total = jnp.where(own_live, jnp.sum(jnp.exp(values - top[:, None]), axis=1), 0.0)
        return top, total

    def merged(tops, totals):
        top = jnp.max(tops, axis=0)
        return top, jnp.sum(totals * jnp.exp(tops - top[None, :]), axis=0)

    teach_top_s, teach_sum_s = local_stats(teach)
    live_row = jnp.broadcast_to(live_value, teach_top_s.shape)
    teach_all = lax.all_gather(jnp.stack([teach_top_s, teach_sum_s, live_row]), "section")
    teach_all, hid_w = lax.optimization_barrier((teach_all, hid_w))
    teach_top, teach_total = merged(teach_all[:, 0], teach_all[:, 1])
    live_count = jnp.sum(teach_all[:, 2, 0])

    part = jnp.einsum("mtw,mrw->mtr", hid_w, rows, preferred_element_type=jnp.float32)
    logits = lax.psum_scatter(part, "z", scatter_dimension=0, tiled=True)[0]

    stud_top_s, stud_sum_s = local_stats(logits)
    stud_all = lax.all_gather(jnp.stack([stud_top_s, stud_sum_s]), "section")
    stud_top, stud_total = merged(stud_all[:, 0], stud_all[:, 1])

    student = jnp.where(own_live, jnp.exp(logits - stud_top[:, None]) / stud_total[:, None], 0.0)
    teach_prob = jnp.where(
        own_live, jnp.exp(teach - teach_top[:, None]) / teach_total[:, None], 0.0
    )
    logit_grad = (block_rows * live_count * (student - teach_prob)).astype(jnp.bfloat16)
    grads = lax.all_gather(logit_grad[None], "z", axis=0, tiled=True)

    contrib_sib = jnp.einsum(
        "mtr,mtw->mrw", grads, hid_w[:, :, col_width:], preferred_element_type=jnp.float32
    ).astype(jnp.bfloat16)
    contrib_got = lax.ppermute(contrib_sib, "core", swap)
    contrib_own = jnp.einsum(
        "mtr,mtw->mrw", grads, hid_w[:, :, :col_width], preferred_element_type=jnp.float32
    ).astype(jnp.bfloat16)

    ghid = jnp.einsum("mtr,mrw->mtw", grads, rows, preferred_element_type=jnp.float32)
    ghid, contrib_got = lax.optimization_barrier((ghid, contrib_got))
    half = n_z // 2
    n_section = lax.axis_size("section")
    summed_a = lax.psum_scatter(ghid[:half], "section", scatter_dimension=1, tiled=True)
    spread = ghid[half:].reshape(n_z - half, n_section, tok_local, -1)
    spread = lax.all_to_all(spread, "section", split_axis=1, concat_axis=1, tiled=True)
    summed_b = jnp.sum(spread, axis=1)
    ghid = jnp.concatenate([summed_a, summed_b], axis=0).astype(jnp.bfloat16)
    ghid = lax.all_to_all(ghid[:, :, None], "z", split_axis=0, concat_axis=2, tiled=True)
    ghid = ghid.reshape(tok_local, n_z, n_core, col_width)
    ghid = jnp.where(odd, ghid[:, :, ::-1, :], ghid)
    grad_hidden = ghid.reshape(1, tok_local, model_width)

    block_range = jnp.arange(blocks, dtype=jnp.int32)[None, :]
    selector = jnp.where(
        (live_flags[:, None] > 0) & (block_ids[:, None] == block_range), 1.0, 0.0
    ).astype(jnp.bfloat16)
    sel_by = selector.reshape(n_z, n_core, blocks)
    sel_own = lax.dynamic_index_in_dim(sel_by, core_at, 1, keepdims=False)
    sel_sib = lax.dynamic_index_in_dim(sel_by, 1 - core_at, 1, keepdims=False)
    grad_head = jnp.einsum("mb,mrw->brw", sel_own, contrib_own, preferred_element_type=jnp.float32)
    grad_head = grad_head + jnp.einsum(
        "mb,mrw->brw", sel_sib, contrib_got, preferred_element_type=jnp.float32
    )
    grad_head = grad_head.astype(jnp.bfloat16).reshape(blocks * block_rows, col_width)
    return (grad_hidden, grad_head)


def solution(mesh):
    n_section, n_dp = mesh.devices.shape
    chips = Mesh(mesh.devices.reshape(n_section, n_dp // 2, 2), ("section", "z", "core"))
    dp = ("z", "core")
    placed = (
        P(dp, "section", None),
        P("section", dp),
        P(None, "section"),
        P(None, "section"),
        P(dp, None, "section"),
    )
    return jax.shard_map(
        local,
        mesh=chips,
        in_specs=placed,
        out_specs=(P(dp, "section", None), P("section", dp)),
        check_vma=False,
    )
```

```python
import jax
import jax.numpy as jnp
from jax import lax
from jax.sharding import Mesh, PartitionSpec as P

neg_fill = -1e30


def local(hidden, head, block_id, block_live, teacher):
    z_at = lax.axis_index("z")
    core_at = lax.axis_index("core")
    n_z = lax.axis_size("z")
    n_core = lax.axis_size("core")
    my_replica = z_at * n_core + core_at
    odd = core_at == 1
    tok_local = hidden.shape[1]
    model_width = hidden.shape[2]
    block_rows = teacher.shape[2]
    col_width = head.shape[1]
    blocks = head.shape[0] // block_rows
    table = head.reshape(blocks, block_rows, col_width)
    block_ids = block_id[:, 0]
    live_flags = block_live[:, 0]
    swap = [(0, 1), (1, 0)]

    ids_by = block_ids.reshape(n_z, n_core)
    own_ids = lax.dynamic_index_in_dim(ids_by, core_at, 1, keepdims=False)
    sib_ids = lax.dynamic_index_in_dim(ids_by, 1 - core_at, 1, keepdims=False)

    pieces = hidden[0].reshape(tok_local, n_z, n_core, col_width)
    pieces = jnp.where(odd, pieces[:, :, ::-1, :], pieces)
    pieces = pieces.reshape(1, tok_local, n_z, n_core * col_width)

    own_rows = jnp.take(table, own_ids, axis=0)
    for_sib = jnp.take(table, sib_ids, axis=0)
    pieces, own_rows, for_sib = lax.optimization_barrier((pieces, own_rows, for_sib))
    sib_rows = lax.ppermute(for_sib, "core", swap)
    pieces = lax.all_to_all(pieces, "z", split_axis=2, concat_axis=0, tiled=True)
    hid_w = lax.all_gather(pieces, "section", axis=1, tiled=True).reshape(n_z, -1, n_core * col_width)
    rows = jnp.concatenate([own_rows, sib_rows], axis=2)

    own_live = lax.dynamic_index_in_dim(live_flags, my_replica, 0, keepdims=False) > 0
    teach = teacher[0].astype(jnp.float32)
    live_value = jnp.where(own_live, 1.0, 0.0).astype(jnp.float32)

    def local_stats(values):
        top = jnp.where(own_live, jnp.max(values, axis=1), neg_fill)
        total = jnp.where(own_live, jnp.sum(jnp.exp(values - top[:, None]), axis=1), 0.0)
        return top, total

    def merged(tops, totals):
        top = jnp.max(tops, axis=0)
        return top, jnp.sum(totals * jnp.exp(tops - top[None, :]), axis=0)

    teach_top_s, teach_sum_s = local_stats(teach)
    live_row = jnp.broadcast_to(live_value, teach_top_s.shape)
    teach_all = lax.all_gather(jnp.stack([teach_top_s, teach_sum_s, live_row]), "section")
    teach_all, hid_w = lax.optimization_barrier((teach_all, hid_w))
    teach_top, teach_total = merged(teach_all[:, 0], teach_all[:, 1])
    live_count = jnp.sum(teach_all[:, 2, 0])

    part = jnp.einsum("mtw,mrw->mtr", hid_w, rows, preferred_element_type=jnp.float32)
    logits = lax.psum_scatter(part, "z", scatter_dimension=0, tiled=True)[0]

    stud_top_s, stud_sum_s = local_stats(logits)
    stud_all = lax.all_gather(jnp.stack([stud_top_s, stud_sum_s]), "section")
    stud_top, stud_total = merged(stud_all[:, 0], stud_all[:, 1])

    student = jnp.where(own_live, jnp.exp(logits - stud_top[:, None]) / stud_total[:, None], 0.0)
    teach_prob = jnp.where(
        own_live, jnp.exp(teach - teach_top[:, None]) / teach_total[:, None], 0.0
    )
    logit_grad = (block_rows * live_count * (student - teach_prob)).astype(jnp.bfloat16)
    grads = lax.all_gather(logit_grad[None], "z", axis=0, tiled=True)

    contrib_sib = jnp.einsum(
        "mtr,mtw->mrw", grads, hid_w[:, :, col_width:], preferred_element_type=jnp.float32
    ).astype(jnp.bfloat16)
    contrib_got = lax.ppermute(contrib_sib, "core", swap)
    contrib_own = jnp.einsum(
        "mtr,mtw->mrw", grads, hid_w[:, :, :col_width], preferred_element_type=jnp.float32
    ).astype(jnp.bfloat16)

    block_range = jnp.arange(blocks, dtype=jnp.int32)[None, :]
    selector = jnp.where(
        (live_flags[:, None] > 0) & (block_ids[:, None] == block_range), 1.0, 0.0
    ).astype(jnp.bfloat16)
    sel_by = selector.reshape(n_z, n_core, blocks)
    sel_own = lax.dynamic_index_in_dim(sel_by, core_at, 1, keepdims=False)
    sel_sib = lax.dynamic_index_in_dim(sel_by, 1 - core_at, 1, keepdims=False)
    grad_head = jnp.einsum("mb,mrw->brw", sel_own, contrib_own, preferred_element_type=jnp.float32)
    grad_head = grad_head + jnp.einsum(
        "mb,mrw->brw", sel_sib, contrib_got, preferred_element_type=jnp.float32
    )
    grad_head = grad_head.astype(jnp.bfloat16).reshape(blocks * block_rows, col_width)
    ghid = jnp.einsum("mtr,mrw->mtw", grads, rows, preferred_element_type=jnp.float32)
    ghid, grad_head = lax.optimization_barrier((ghid, grad_head))
    ghid = lax.psum_scatter(ghid, "section", scatter_dimension=1, tiled=True).astype(jnp.bfloat16)
    ghid = lax.all_to_all(ghid[:, :, None], "z", split_axis=0, concat_axis=2, tiled=True)
    ghid = ghid.reshape(tok_local, n_z, n_core, col_width)
    ghid = jnp.where(odd, ghid[:, :, ::-1, :], ghid)
    grad_hidden = ghid.reshape(1, tok_local, model_width)

    return (grad_hidden, grad_head)


def solution(mesh):
    n_section, n_dp = mesh.devices.shape
    chips = Mesh(mesh.devices.reshape(n_section, n_dp // 2, 2), ("section", "z", "core"))
    dp = ("z", "core")
    placed = (
        P(dp, "section", None),
        P("section", dp),
        P(None, "section"),
        P(None, "section"),
        P(dp, None, "section"),
    )
    return jax.shard_map(
        local,
        mesh=chips,
        in_specs=placed,
        out_specs=(P(dp, "section", None), P("section", dp)),
        check_vma=False,
    )
```

```python
import jax
import jax.numpy as jnp
from jax import lax
from jax.sharding import Mesh, PartitionSpec as P

neg_fill = -1e30


def local(hidden, head, block_id, block_live, teacher):
    z_at = lax.axis_index("z")
    core_at = lax.axis_index("core")
    n_z = lax.axis_size("z")
    n_core = lax.axis_size("core")
    my_replica = z_at * n_core + core_at
    odd = core_at == 1
    tok_local = hidden.shape[1]
    model_width = hidden.shape[2]
    block_rows = teacher.shape[2]
    col_width = head.shape[1]
    blocks = head.shape[0] // block_rows
    table = head.reshape(blocks, block_rows, col_width)
    block_ids = block_id[:, 0]
    live_flags = block_live[:, 0]
    swap = [(0, 1), (1, 0)]

    ids_by = block_ids.reshape(n_z, n_core)
    own_ids = lax.dynamic_index_in_dim(ids_by, core_at, 1, keepdims=False)
    sib_ids = lax.dynamic_index_in_dim(ids_by, 1 - core_at, 1, keepdims=False)

    pieces = hidden[0].reshape(tok_local, n_z, n_core, col_width)
    pieces = jnp.where(odd, pieces[:, :, ::-1, :], pieces)
    pieces = pieces.transpose(1, 0, 2, 3).reshape(n_z, tok_local, n_core * col_width)
    arrived = [lax.dynamic_index_in_dim(pieces, z_at, 0, keepdims=False)]
    for k in range(1, n_z):
        sent = lax.dynamic_index_in_dim(pieces, (z_at + k) % n_z, 0, keepdims=False)
        arrived.append(lax.ppermute(sent, "z", [(j, (j + k) % n_z) for j in range(n_z)]))
    order = (z_at - jnp.arange(n_z, dtype=jnp.int32)) % n_z
    pieces = jnp.take(jnp.stack(arrived), order, axis=0)
    hid_w = lax.all_gather(pieces, "section", axis=1, tiled=True)

    own_rows = jnp.take(table, own_ids, axis=0)
    sib_rows = lax.ppermute(jnp.take(table, sib_ids, axis=0), "core", swap)
    rows = jnp.concatenate([own_rows, sib_rows], axis=2)

    own_live = lax.dynamic_index_in_dim(live_flags, my_replica, 0, keepdims=False) > 0
    teach = teacher[0].astype(jnp.float32)
    live_value = jnp.where(own_live, 1.0, 0.0).astype(jnp.float32)

    def local_stats(values):
        top = jnp.where(own_live, jnp.max(values, axis=1), neg_fill)
        total = jnp.where(own_live, jnp.sum(jnp.exp(values - top[:, None]), axis=1), 0.0)
        return top, total

    def merged(tops, totals):
        top = jnp.max(tops, axis=0)
        return top, jnp.sum(totals * jnp.exp(tops - top[None, :]), axis=0)

    teach_top_s, teach_sum_s = local_stats(teach)
    live_row = jnp.broadcast_to(live_value, teach_top_s.shape)
    teach_all = lax.all_gather(jnp.stack([teach_top_s, teach_sum_s, live_row]), "section")
    teach_all, hid_w = lax.optimization_barrier((teach_all, hid_w))
    teach_top, teach_total = merged(teach_all[:, 0], teach_all[:, 1])
    live_count = jnp.sum(teach_all[:, 2, 0])

    part = jnp.einsum("mtw,mrw->mtr", hid_w, rows, preferred_element_type=jnp.float32)
    logits = lax.psum_scatter(part, "z", scatter_dimension=0, tiled=True)[0]

    stud_top_s, stud_sum_s = local_stats(logits)
    stud_all = lax.all_gather(jnp.stack([stud_top_s, stud_sum_s]), "section")
    stud_top, stud_total = merged(stud_all[:, 0], stud_all[:, 1])

    student = jnp.where(own_live, jnp.exp(logits - stud_top[:, None]) / stud_total[:, None], 0.0)
    teach_prob = jnp.where(
        own_live, jnp.exp(teach - teach_top[:, None]) / teach_total[:, None], 0.0
    )
    logit_grad = (block_rows * live_count * (student - teach_prob)).astype(jnp.bfloat16)
    grads = lax.all_gather(logit_grad[None], "z", axis=0, tiled=True)

    contrib_sib = jnp.einsum(
        "mtr,mtw->mrw", grads, hid_w[:, :, col_width:], preferred_element_type=jnp.float32
    ).astype(jnp.bfloat16)
    contrib_got = lax.ppermute(contrib_sib, "core", swap)
    contrib_own = jnp.einsum(
        "mtr,mtw->mrw", grads, hid_w[:, :, :col_width], preferred_element_type=jnp.float32
    ).astype(jnp.bfloat16)

    ghid = jnp.einsum("mtr,mrw->mtw", grads, rows, preferred_element_type=jnp.float32)
    ghid, contrib_got = lax.optimization_barrier((ghid, contrib_got))
    ghid = lax.psum_scatter(ghid, "section", scatter_dimension=1, tiled=True).astype(jnp.bfloat16)
    ghid = lax.all_to_all(ghid[:, :, None], "z", split_axis=0, concat_axis=2, tiled=True)
    ghid = ghid.reshape(tok_local, n_z, n_core, col_width)
    ghid = jnp.where(odd, ghid[:, :, ::-1, :], ghid)
    grad_hidden = ghid.reshape(1, tok_local, model_width)

    block_range = jnp.arange(blocks, dtype=jnp.int32)[None, :]
    selector = jnp.where(
        (live_flags[:, None] > 0) & (block_ids[:, None] == block_range), 1.0, 0.0
    ).astype(jnp.bfloat16)
    sel_by = selector.reshape(n_z, n_core, blocks)
    sel_own = lax.dynamic_index_in_dim(sel_by, core_at, 1, keepdims=False)
    sel_sib = lax.dynamic_index_in_dim(sel_by, 1 - core_at, 1, keepdims=False)
    grad_head = jnp.einsum("mb,mrw->brw", sel_own, contrib_own, preferred_element_type=jnp.float32)
    grad_head = grad_head + jnp.einsum(
        "mb,mrw->brw", sel_sib, contrib_got, preferred_element_type=jnp.float32
    )
    grad_head = grad_head.astype(jnp.bfloat16).reshape(blocks * block_rows, col_width)
    return (grad_hidden, grad_head)


def solution(mesh):
    n_section, n_dp = mesh.devices.shape
    chips = Mesh(mesh.devices.reshape(n_section, n_dp // 2, 2), ("section", "z", "core"))
    dp = ("z", "core")
    placed = (
        P(dp, "section", None),
        P("section", dp),
        P(None, "section"),
        P(None, "section"),
        P(dp, None, "section"),
    )
    return jax.shard_map(
        local,
        mesh=chips,
        in_specs=placed,
        out_specs=(P(dp, "section", None), P("section", dp)),
        check_vma=False,
    )
```

```python
import jax
import jax.numpy as jnp
from jax import lax
from jax.sharding import Mesh, PartitionSpec as P

neg_fill = -1e30


def local(hidden, head, block_id, block_live, teacher):
    z_at = lax.axis_index("z")
    core_at = lax.axis_index("core")
    n_z = lax.axis_size("z")
    n_core = lax.axis_size("core")
    my_replica = z_at * n_core + core_at
    odd = core_at == 1
    tok_local = hidden.shape[1]
    model_width = hidden.shape[2]
    block_rows = teacher.shape[2]
    col_width = head.shape[1]
    blocks = head.shape[0] // block_rows
    table = head.reshape(blocks, block_rows, col_width)
    block_ids = block_id[:, 0]
    live_flags = block_live[:, 0]
    swap = [(0, 1), (1, 0)]

    ids_by = block_ids.reshape(n_z, n_core)
    own_ids = lax.dynamic_index_in_dim(ids_by, core_at, 1, keepdims=False)
    sib_ids = lax.dynamic_index_in_dim(ids_by, 1 - core_at, 1, keepdims=False)

    pieces = hidden[0].reshape(tok_local, n_z, n_core, col_width)
    pieces = jnp.where(odd, pieces[:, :, ::-1, :], pieces)
    pieces = pieces.reshape(1, tok_local, n_z, n_core * col_width)
    pieces = lax.all_to_all(pieces, "z", split_axis=2, concat_axis=0, tiled=True)
    hid_w = lax.all_gather(pieces, "section", axis=1, tiled=True).reshape(n_z, -1, n_core * col_width)

    own_rows = jnp.take(table, own_ids, axis=0)
    sib_rows = lax.ppermute(jnp.take(table, sib_ids, axis=0), "core", swap)
    rows = jnp.concatenate([own_rows, sib_rows], axis=2)

    own_live = lax.dynamic_index_in_dim(live_flags, my_replica, 0, keepdims=False) > 0
    teach = teacher[0].astype(jnp.float32)
    live_value = jnp.where(own_live, 1.0, 0.0).astype(jnp.float32)

    def local_stats(values):
        top = jnp.where(own_live, jnp.max(values, axis=1), neg_fill)
        total = jnp.where(own_live, jnp.sum(jnp.exp(values - top[:, None]), axis=1), 0.0)
        return top, total

    def merged(tops, totals):
        top = jnp.max(tops, axis=0)
        return top, jnp.sum(totals * jnp.exp(tops - top[None, :]), axis=0)

    teach_top_s, teach_sum_s = local_stats(teach)
    live_row = jnp.broadcast_to(live_value, teach_top_s.shape)
    teach_all = lax.all_gather(jnp.stack([teach_top_s, teach_sum_s, live_row]), "section")
    teach_all, hid_w = lax.optimization_barrier((teach_all, hid_w))
    teach_top, teach_total = merged(teach_all[:, 0], teach_all[:, 1])
    live_count = jnp.sum(teach_all[:, 2, 0])

    part = jnp.einsum("mtw,mrw->mtr", hid_w, rows, preferred_element_type=jnp.float32)
    logits = lax.psum_scatter(part, "z", scatter_dimension=0, tiled=True)[0]

    stud_top_s, stud_sum_s = local_stats(logits)
    stud_all = lax.all_gather(jnp.stack([stud_top_s, stud_sum_s]), "section")
    stud_top, stud_total = merged(stud_all[:, 0], stud_all[:, 1])

    student = jnp.where(own_live, jnp.exp(logits - stud_top[:, None]) / stud_total[:, None], 0.0)
    teach_prob = jnp.where(
        own_live, jnp.exp(teach - teach_top[:, None]) / teach_total[:, None], 0.0
    )
    logit_grad = (block_rows * live_count * (student - teach_prob)).astype(jnp.bfloat16)
    grads = lax.all_gather(logit_grad[None], "z", axis=0, tiled=True)

    ghid = jnp.einsum("mtr,mrw->mtw", grads, rows, preferred_element_type=jnp.float32)
    ghid, grads = lax.optimization_barrier((ghid, grads))
    contrib_sib = jnp.einsum(
        "mtr,mtw->mrw", grads, hid_w[:, :, col_width:], preferred_element_type=jnp.float32
    ).astype(jnp.bfloat16)
    contrib_got = lax.ppermute(contrib_sib, "core", swap)
    contrib_own = jnp.einsum(
        "mtr,mtw->mrw", grads, hid_w[:, :, :col_width], preferred_element_type=jnp.float32
    ).astype(jnp.bfloat16)

    ghid = lax.psum_scatter(ghid, "section", scatter_dimension=1, tiled=True).astype(jnp.bfloat16)
    ghid = lax.all_to_all(ghid[:, :, None], "z", split_axis=0, concat_axis=2, tiled=True)
    ghid = ghid.reshape(tok_local, n_z, n_core, col_width)
    ghid = jnp.where(odd, ghid[:, :, ::-1, :], ghid)
    grad_hidden = ghid.reshape(1, tok_local, model_width)

    block_range = jnp.arange(blocks, dtype=jnp.int32)[None, :]
    selector = jnp.where(
        (live_flags[:, None] > 0) & (block_ids[:, None] == block_range), 1.0, 0.0
    ).astype(jnp.bfloat16)
    sel_by = selector.reshape(n_z, n_core, blocks)
    sel_own = lax.dynamic_index_in_dim(sel_by, core_at, 1, keepdims=False)
    sel_sib = lax.dynamic_index_in_dim(sel_by, 1 - core_at, 1, keepdims=False)
    n_own = contrib_own.shape[0]
    grad_head = jnp.dot(
        sel_own.T, contrib_own.reshape(n_own, -1), preferred_element_type=jnp.float32
    ) + jnp.dot(sel_sib.T, contrib_got.reshape(n_own, -1), preferred_element_type=jnp.float32)
    grad_head = grad_head.astype(jnp.bfloat16).reshape(blocks * block_rows, col_width)
    return (grad_hidden, grad_head)


def solution(mesh):
    n_section, n_dp = mesh.devices.shape
    chips = Mesh(mesh.devices.reshape(n_section, n_dp // 2, 2), ("section", "z", "core"))
    dp = ("z", "core")
    placed = (
        P(dp, "section", None),
        P("section", dp),
        P(None, "section"),
        P(None, "section"),
        P(dp, None, "section"),
    )
    return jax.shard_map(
        local,
        mesh=chips,
        in_specs=placed,
        out_specs=(P(dp, "section", None), P("section", dp)),
        check_vma=False,
    )
```

```python
import jax
import jax.numpy as jnp
from jax import lax
from jax.sharding import Mesh, PartitionSpec as P

neg_fill = -1e30


def local(hidden, head, block_id, block_live, teacher):
    z_at = lax.axis_index("z")
    core_at = lax.axis_index("core")
    n_z = lax.axis_size("z")
    n_core = lax.axis_size("core")
    my_replica = z_at * n_core + core_at
    odd = core_at == 1
    tok_local = hidden.shape[1]
    model_width = hidden.shape[2]
    block_rows = teacher.shape[2]
    col_width = head.shape[1]
    blocks = head.shape[0] // block_rows
    table = head.reshape(blocks, block_rows, col_width)
    block_ids = block_id[:, 0]
    live_flags = block_live[:, 0]
    swap = [(0, 1), (1, 0)]

    ids_by = block_ids.reshape(n_z, n_core)
    own_ids = lax.dynamic_index_in_dim(ids_by, core_at, 1, keepdims=False)
    sib_ids = lax.dynamic_index_in_dim(ids_by, 1 - core_at, 1, keepdims=False)

    pieces = hidden[0].reshape(tok_local, n_z, n_core, col_width)
    pieces = jnp.where(odd, pieces[:, :, ::-1, :], pieces)
    pieces = pieces.reshape(1, tok_local, n_z, n_core * col_width)
    pieces = lax.all_to_all(pieces, "z", split_axis=2, concat_axis=0, tiled=True)
    hid_w = lax.all_gather(pieces, "section", axis=1, tiled=True).reshape(n_z, -1, n_core * col_width)

    own_rows = jnp.take(table, own_ids, axis=0)
    sib_rows = lax.ppermute(jnp.take(table, sib_ids, axis=0), "core", swap)
    rows = jnp.concatenate([own_rows, sib_rows], axis=2)

    own_live = lax.dynamic_index_in_dim(live_flags, my_replica, 0, keepdims=False) > 0
    teach = teacher[0].astype(jnp.float32)
    live_value = jnp.where(own_live, 1.0, 0.0).astype(jnp.float32)

    def local_stats(values):
        top = jnp.where(own_live, jnp.max(values, axis=1), neg_fill)
        total = jnp.where(own_live, jnp.sum(jnp.exp(values - top[:, None]), axis=1), 0.0)
        return top, total

    def merged(tops, totals):
        top = jnp.max(tops, axis=0)
        return top, jnp.sum(totals * jnp.exp(tops - top[None, :]), axis=0)

    teach_top_s, teach_sum_s = local_stats(teach)
    live_row = jnp.broadcast_to(live_value, teach_top_s.shape)
    teach_all = lax.all_gather(jnp.stack([teach_top_s, teach_sum_s, live_row]), "section")
    teach_all, hid_w = lax.optimization_barrier((teach_all, hid_w))
    teach_top, teach_total = merged(teach_all[:, 0], teach_all[:, 1])
    live_count = jnp.sum(teach_all[:, 2, 0])

    part = jnp.einsum("mtw,mrw->mtr", hid_w, rows, preferred_element_type=jnp.float32)
    logits = lax.psum_scatter(part, "z", scatter_dimension=0, tiled=True)[0]

    stud_top_s, stud_sum_s = local_stats(logits)
    stud_all = lax.all_gather(jnp.stack([stud_top_s, stud_sum_s]), "section")
    stud_top, stud_total = merged(stud_all[:, 0], stud_all[:, 1])

    student = jnp.where(own_live, jnp.exp(logits - stud_top[:, None]) / stud_total[:, None], 0.0)
    teach_prob = jnp.where(
        own_live, jnp.exp(teach - teach_top[:, None]) / teach_total[:, None], 0.0
    )
    logit_grad = (block_rows * live_count * (student - teach_prob)).astype(jnp.bfloat16)
    grads = lax.all_gather(logit_grad[None], "z", axis=0, tiled=True)

    ghid = jnp.einsum("mtr,mrw->mtw", grads, rows, preferred_element_type=jnp.float32)
    ghid, grads = lax.optimization_barrier((ghid, grads))
    contrib_sib = jnp.einsum(
        "mtr,mtw->mrw", grads, hid_w[:, :, col_width:], preferred_element_type=jnp.float32
    ).astype(jnp.bfloat16)
    contrib_got = lax.ppermute(contrib_sib, "core", swap)
    contrib_own = jnp.einsum(
        "mtr,mtw->mrw", grads, hid_w[:, :, :col_width], preferred_element_type=jnp.float32
    ).astype(jnp.bfloat16)

    block_range = jnp.arange(blocks, dtype=jnp.int32)[None, :]
    selector = jnp.where(
        (live_flags[:, None] > 0) & (block_ids[:, None] == block_range), 1.0, 0.0
    ).astype(jnp.bfloat16)
    sel_by = selector.reshape(n_z, n_core, blocks)
    sel_own = lax.dynamic_index_in_dim(sel_by, core_at, 1, keepdims=False)
    sel_sib = lax.dynamic_index_in_dim(sel_by, 1 - core_at, 1, keepdims=False)
    n_own = contrib_own.shape[0]
    grad_head = jnp.dot(
        sel_own.T, contrib_own.reshape(n_own, -1), preferred_element_type=jnp.float32
    ) + jnp.dot(sel_sib.T, contrib_got.reshape(n_own, -1), preferred_element_type=jnp.float32)
    grad_head = grad_head.astype(jnp.bfloat16)
    ghid = lax.psum_scatter(ghid, "section", scatter_dimension=1, tiled=True)
    ghid, grad_head = lax.optimization_barrier((ghid, grad_head))
    grad_head = grad_head.reshape(blocks * block_rows, col_width)
    ghid = ghid.astype(jnp.bfloat16)
    ghid = lax.all_to_all(ghid[:, :, None], "z", split_axis=0, concat_axis=2, tiled=True)
    ghid = ghid.reshape(tok_local, n_z, n_core, col_width)
    ghid = jnp.where(odd, ghid[:, :, ::-1, :], ghid)
    grad_hidden = ghid.reshape(1, tok_local, model_width)

    return (grad_hidden, grad_head)


def solution(mesh):
    n_section, n_dp = mesh.devices.shape
    chips = Mesh(mesh.devices.reshape(n_section, n_dp // 2, 2), ("section", "z", "core"))
    dp = ("z", "core")
    placed = (
        P(dp, "section", None),
        P("section", dp),
        P(None, "section"),
        P(None, "section"),
        P(dp, None, "section"),
    )
    return jax.shard_map(
        local,
        mesh=chips,
        in_specs=placed,
        out_specs=(P(dp, "section", None), P("section", dp)),
        check_vma=False,
    )
```

```python
import jax
import jax.numpy as jnp
from jax import lax
from jax.sharding import Mesh, PartitionSpec as P

neg_fill = -1e30


def local(hidden, head, block_id, block_live, teacher):
    z_at = lax.axis_index("z")
    core_at = lax.axis_index("core")
    n_z = lax.axis_size("z")
    n_core = lax.axis_size("core")
    my_replica = z_at * n_core + core_at
    odd = core_at == 1
    tok_local = hidden.shape[1]
    model_width = hidden.shape[2]
    block_rows = teacher.shape[2]
    col_width = head.shape[1]
    blocks = head.shape[0] // block_rows
    table = head.reshape(blocks, block_rows, col_width)
    block_ids = block_id[:, 0]
    live_flags = block_live[:, 0]
    swap = [(0, 1), (1, 0)]

    ids_by = block_ids.reshape(n_z, n_core)
    own_ids = lax.dynamic_index_in_dim(ids_by, core_at, 1, keepdims=False)
    sib_ids = lax.dynamic_index_in_dim(ids_by, 1 - core_at, 1, keepdims=False)

    pieces = hidden.reshape(1, tok_local, n_z, n_core * col_width)
    pieces = lax.all_to_all(pieces, "z", split_axis=2, concat_axis=0, tiled=True)
    hid_w = lax.all_gather(pieces, "section", axis=1, tiled=True).reshape(n_z, -1, n_core * col_width)

    own_rows = jnp.take(table, own_ids, axis=0)
    sib_rows = lax.ppermute(jnp.take(table, sib_ids, axis=0), "core", swap)
    rows = jnp.stack([own_rows, sib_rows], axis=2)
    rows = jnp.where(odd, rows[:, :, ::-1], rows).reshape(n_z, block_rows, n_core * col_width)

    own_live = lax.dynamic_index_in_dim(live_flags, my_replica, 0, keepdims=False) > 0
    teach = teacher[0].astype(jnp.float32)
    live_value = jnp.where(own_live, 1.0, 0.0).astype(jnp.float32)

    def local_stats(values):
        top = jnp.where(own_live, jnp.max(values, axis=1), neg_fill)
        total = jnp.where(own_live, jnp.sum(jnp.exp(values - top[:, None]), axis=1), 0.0)
        return top, total

    def merged(tops, totals):
        top = jnp.max(tops, axis=0)
        return top, jnp.sum(totals * jnp.exp(tops - top[None, :]), axis=0)

    teach_top_s, teach_sum_s = local_stats(teach)
    live_row = jnp.broadcast_to(live_value, teach_top_s.shape)
    teach_all = lax.all_gather(jnp.stack([teach_top_s, teach_sum_s, live_row]), "section")
    teach_all, hid_w = lax.optimization_barrier((teach_all, hid_w))
    teach_top, teach_total = merged(teach_all[:, 0], teach_all[:, 1])
    live_count = jnp.sum(teach_all[:, 2, 0])

    part = jnp.einsum("mtw,mrw->mtr", hid_w, rows, preferred_element_type=jnp.float32)
    logits = lax.psum_scatter(part, "z", scatter_dimension=0, tiled=True)[0]

    stud_top_s, stud_sum_s = local_stats(logits)
    stud_all = lax.all_gather(jnp.stack([stud_top_s, stud_sum_s]), "section")
    stud_top, stud_total = merged(stud_all[:, 0], stud_all[:, 1])

    student = jnp.where(own_live, jnp.exp(logits - stud_top[:, None]) / stud_total[:, None], 0.0)
    teach_prob = jnp.where(
        own_live, jnp.exp(teach - teach_top[:, None]) / teach_total[:, None], 0.0
    )
    logit_grad = (block_rows * live_count * (student - teach_prob)).astype(jnp.bfloat16)
    grads = lax.all_gather(logit_grad[None], "z", axis=0, tiled=True)

    ghid = jnp.einsum("mtr,mrw->mtw", grads, rows, preferred_element_type=jnp.float32)
    ghid, grads = lax.optimization_barrier((ghid, grads))
    contrib_sib = jnp.einsum(
        "mtr,mtw->mrw", grads, lax.dynamic_slice_in_dim(hid_w, (1 - core_at) * col_width, col_width, 2), preferred_element_type=jnp.float32
    ).astype(jnp.bfloat16)
    contrib_got = lax.ppermute(contrib_sib, "core", swap)
    contrib_own = jnp.einsum(
        "mtr,mtw->mrw", grads, lax.dynamic_slice_in_dim(hid_w, core_at * col_width, col_width, 2), preferred_element_type=jnp.float32
    ).astype(jnp.bfloat16)

    block_range = jnp.arange(blocks, dtype=jnp.int32)[None, :]
    selector = jnp.where(
        (live_flags[:, None] > 0) & (block_ids[:, None] == block_range), 1.0, 0.0
    ).astype(jnp.bfloat16)
    sel_by = selector.reshape(n_z, n_core, blocks)
    sel_own = lax.dynamic_index_in_dim(sel_by, core_at, 1, keepdims=False)
    sel_sib = lax.dynamic_index_in_dim(sel_by, 1 - core_at, 1, keepdims=False)
    n_own = contrib_own.shape[0]
    grad_head = jnp.dot(
        sel_own.T, contrib_own.reshape(n_own, -1), preferred_element_type=jnp.float32
    ) + jnp.dot(sel_sib.T, contrib_got.reshape(n_own, -1), preferred_element_type=jnp.float32)
    grad_head = grad_head.astype(jnp.bfloat16)
    ghid = lax.psum_scatter(ghid, "section", scatter_dimension=1, tiled=True)
    ghid, grad_head = lax.optimization_barrier((ghid, grad_head))
    grad_head = grad_head.reshape(blocks * block_rows, col_width)
    ghid = ghid.astype(jnp.bfloat16)
    ghid = lax.all_to_all(ghid[:, :, None], "z", split_axis=0, concat_axis=2, tiled=True)
    grad_hidden = ghid.reshape(1, tok_local, model_width)

    return (grad_hidden, grad_head)


def solution(mesh):
    n_section, n_dp = mesh.devices.shape
    chips = Mesh(mesh.devices.reshape(n_section, n_dp // 2, 2), ("section", "z", "core"))
    dp = ("z", "core")
    placed = (
        P(dp, "section", None),
        P("section", dp),
        P(None, "section"),
        P(None, "section"),
        P(dp, None, "section"),
    )
    return jax.shard_map(
        local,
        mesh=chips,
        in_specs=placed,
        out_specs=(P(dp, "section", None), P("section", dp)),
        check_vma=False,
    )
```

```python
import jax
import jax.numpy as jnp
from jax import lax
from jax.sharding import Mesh, PartitionSpec as P

neg_fill = -1e30


def local(hidden, head, block_id, block_live, teacher):
    z_at = lax.axis_index("z")
    core_at = lax.axis_index("core")
    n_z = lax.axis_size("z")
    n_core = lax.axis_size("core")
    my_replica = z_at * n_core + core_at
    tok_local = hidden.shape[1]
    model_width = hidden.shape[2]
    block_rows = teacher.shape[2]
    col_width = head.shape[1]
    blocks = head.shape[0] // block_rows
    table = head.reshape(blocks, block_rows, col_width)
    block_ids = block_id[:, 0]
    live_flags = block_live[:, 0]
    swap = [(0, 1), (1, 0)]

    ids_by = block_ids.reshape(n_z, n_core)
    own_ids = lax.dynamic_index_in_dim(ids_by, core_at, 1, keepdims=False)
    sib_ids = lax.dynamic_index_in_dim(ids_by, 1 - core_at, 1, keepdims=False)

    pair_swap = jnp.arange(n_z * n_core, dtype=jnp.int32) ^ core_at
    pieces = jnp.take(hidden[0].reshape(tok_local, n_z * n_core, col_width), pair_swap, axis=1)
    pieces = pieces.reshape(1, tok_local, n_z, n_core * col_width)
    pieces = lax.all_to_all(pieces, "z", split_axis=2, concat_axis=0, tiled=True)
    hid_w = lax.all_gather(pieces, "section", axis=1, tiled=True).reshape(n_z, -1, n_core * col_width)

    own_rows = jnp.take(table, own_ids, axis=0)
    sib_rows = lax.ppermute(jnp.take(table, sib_ids, axis=0), "core", swap)
    rows = jnp.concatenate([own_rows, sib_rows], axis=2)

    own_live = lax.dynamic_index_in_dim(live_flags, my_replica, 0, keepdims=False) > 0
    teach = teacher[0].astype(jnp.float32)
    live_value = jnp.where(own_live, 1.0, 0.0).astype(jnp.float32)

    def local_stats(values):
        top = jnp.where(own_live, jnp.max(values, axis=1), neg_fill)
        total = jnp.where(own_live, jnp.sum(jnp.exp(values - top[:, None]), axis=1), 0.0)
        return top, total

    def merged(tops, totals):
        top = jnp.max(tops, axis=0)
        return top, jnp.sum(totals * jnp.exp(tops - top[None, :]), axis=0)

    teach_top_s, teach_sum_s = local_stats(teach)
    live_row = jnp.broadcast_to(live_value, teach_top_s.shape)
    teach_all = lax.all_gather(jnp.stack([teach_top_s, teach_sum_s, live_row]), "section")
    teach_all, hid_w = lax.optimization_barrier((teach_all, hid_w))
    teach_top, teach_total = merged(teach_all[:, 0], teach_all[:, 1])
    live_count = jnp.sum(teach_all[:, 2, 0])

    part = jnp.einsum("mtw,mrw->mtr", hid_w, rows, preferred_element_type=jnp.float32)
    logits = lax.psum_scatter(part, "z", scatter_dimension=0, tiled=True)[0]

    stud_top_s, stud_sum_s = local_stats(logits)
    stud_all = lax.all_gather(jnp.stack([stud_top_s, stud_sum_s]), "section")
    stud_top, stud_total = merged(stud_all[:, 0], stud_all[:, 1])

    student = jnp.where(own_live, jnp.exp(logits - stud_top[:, None]) / stud_total[:, None], 0.0)
    teach_prob = jnp.where(
        own_live, jnp.exp(teach - teach_top[:, None]) / teach_total[:, None], 0.0
    )
    logit_grad = (block_rows * live_count * (student - teach_prob)).astype(jnp.bfloat16)
    grads = lax.all_gather(logit_grad[None], "z", axis=0, tiled=True)

    ghid = jnp.einsum("mtr,mrw->mtw", grads, rows, preferred_element_type=jnp.float32)
    ghid, grads = lax.optimization_barrier((ghid, grads))
    contrib_sib = jnp.einsum(
        "mtr,mtw->mrw", grads, hid_w[:, :, col_width:], preferred_element_type=jnp.float32
    ).astype(jnp.bfloat16)
    contrib_got = lax.ppermute(contrib_sib, "core", swap)
    contrib_own = jnp.einsum(
        "mtr,mtw->mrw", grads, hid_w[:, :, :col_width], preferred_element_type=jnp.float32
    ).astype(jnp.bfloat16)

    block_range = jnp.arange(blocks, dtype=jnp.int32)[None, :]
    selector = jnp.where(
        (live_flags[:, None] > 0) & (block_ids[:, None] == block_range), 1.0, 0.0
    ).astype(jnp.bfloat16)
    sel_by = selector.reshape(n_z, n_core, blocks)
    sel_own = lax.dynamic_index_in_dim(sel_by, core_at, 1, keepdims=False)
    sel_sib = lax.dynamic_index_in_dim(sel_by, 1 - core_at, 1, keepdims=False)
    n_own = contrib_own.shape[0]
    grad_head = jnp.dot(
        sel_own.T, contrib_own.reshape(n_own, -1), preferred_element_type=jnp.float32
    ) + jnp.dot(sel_sib.T, contrib_got.reshape(n_own, -1), preferred_element_type=jnp.float32)
    grad_head = grad_head.astype(jnp.bfloat16)
    ghid = lax.psum_scatter(ghid, "section", scatter_dimension=1, tiled=True)
    ghid, grad_head = lax.optimization_barrier((ghid, grad_head))
    grad_head = grad_head.reshape(blocks * block_rows, col_width)
    ghid = ghid.astype(jnp.bfloat16)
    ghid = lax.all_to_all(ghid[:, :, None], "z", split_axis=0, concat_axis=2, tiled=True)
    ghid = jnp.take(ghid.reshape(tok_local, n_z * n_core, col_width), pair_swap, axis=1)
    grad_hidden = ghid.reshape(1, tok_local, model_width)

    return (grad_hidden, grad_head)


def solution(mesh):
    n_section, n_dp = mesh.devices.shape
    chips = Mesh(mesh.devices.reshape(n_section, n_dp // 2, 2), ("section", "z", "core"))
    dp = ("z", "core")
    placed = (
        P(dp, "section", None),
        P("section", dp),
        P(None, "section"),
        P(None, "section"),
        P(dp, None, "section"),
    )
    return jax.shard_map(
        local,
        mesh=chips,
        in_specs=placed,
        out_specs=(P(dp, "section", None), P("section", dp)),
        check_vma=False,
    )
```

```python
import jax
import jax.numpy as jnp
from jax import lax
from jax.sharding import Mesh, PartitionSpec as P

neg_fill = -1e30


def local(hidden, head, block_id, block_live, teacher):
    z_at = lax.axis_index("z")
    core_at = lax.axis_index("core")
    n_z = lax.axis_size("z")
    n_core = lax.axis_size("core")
    my_replica = z_at * n_core + core_at
    tok_local = hidden.shape[1]
    model_width = hidden.shape[2]
    block_rows = teacher.shape[2]
    col_width = head.shape[1]
    blocks = head.shape[0] // block_rows
    table = head.reshape(blocks, block_rows, col_width)
    block_ids = block_id[:, 0]
    live_flags = block_live[:, 0]
    swap = [(0, 1), (1, 0)]

    ids_by = block_ids.reshape(n_z, n_core)
    own_ids = lax.dynamic_index_in_dim(ids_by, core_at, 1, keepdims=False)
    sib_ids = lax.dynamic_index_in_dim(ids_by, 1 - core_at, 1, keepdims=False)

    pair_swap = jnp.arange(n_z * n_core, dtype=jnp.int32) ^ core_at
    pieces = jnp.take(hidden[0].reshape(tok_local, n_z * n_core, col_width), pair_swap, axis=1)
    pieces = pieces.reshape(1, tok_local, n_z, n_core * col_width)
    pieces = lax.all_to_all(pieces, "z", split_axis=2, concat_axis=0, tiled=True)

    own_rows = jnp.take(table, own_ids, axis=0)
    for_sib = jnp.take(table, sib_ids, axis=0)
    pieces, own_rows, for_sib = lax.optimization_barrier((pieces, own_rows, for_sib))
    hid_w = lax.all_gather(pieces, "section", axis=1, tiled=True).reshape(n_z, -1, n_core * col_width)
    sib_rows = lax.ppermute(for_sib, "core", swap)
    rows = jnp.concatenate([own_rows, sib_rows], axis=2)

    own_live = lax.dynamic_index_in_dim(live_flags, my_replica, 0, keepdims=False) > 0
    teach = teacher[0].astype(jnp.float32)
    live_value = jnp.where(own_live, 1.0, 0.0).astype(jnp.float32)

    def local_stats(values):
        top = jnp.where(own_live, jnp.max(values, axis=1), neg_fill)
        total = jnp.where(own_live, jnp.sum(jnp.exp(values - top[:, None]), axis=1), 0.0)
        return top, total

    def merged(tops, totals):
        top = jnp.max(tops, axis=0)
        return top, jnp.sum(totals * jnp.exp(tops - top[None, :]), axis=0)

    teach_top_s, teach_sum_s = local_stats(teach)
    live_row = jnp.broadcast_to(live_value, teach_top_s.shape)
    teach_all = lax.all_gather(jnp.stack([teach_top_s, teach_sum_s, live_row]), "section")
    teach_all, hid_w = lax.optimization_barrier((teach_all, hid_w))
    teach_top, teach_total = merged(teach_all[:, 0], teach_all[:, 1])
    live_count = jnp.sum(teach_all[:, 2, 0])

    part = jnp.einsum("mtw,mrw->mtr", hid_w, rows, preferred_element_type=jnp.float32)
    logits = lax.psum_scatter(part, "z", scatter_dimension=0, tiled=True)[0]

    stud_top_s, stud_sum_s = local_stats(logits)
    stud_all = lax.all_gather(jnp.stack([stud_top_s, stud_sum_s]), "section")
    stud_top, stud_total = merged(stud_all[:, 0], stud_all[:, 1])

    student = jnp.where(own_live, jnp.exp(logits - stud_top[:, None]) / stud_total[:, None], 0.0)
    teach_prob = jnp.where(
        own_live, jnp.exp(teach - teach_top[:, None]) / teach_total[:, None], 0.0
    )
    logit_grad = (block_rows * live_count * (student - teach_prob)).astype(jnp.bfloat16)
    grads = lax.all_gather(logit_grad[None], "z", axis=0, tiled=True)

    ghid = jnp.einsum("mtr,mrw->mtw", grads, rows, preferred_element_type=jnp.float32)
    ghid, grads = lax.optimization_barrier((ghid, grads))
    contrib_sib = jnp.einsum(
        "mtr,mtw->mrw", grads, hid_w[:, :, col_width:], preferred_element_type=jnp.float32
    ).astype(jnp.bfloat16)
    contrib_got = lax.ppermute(contrib_sib, "core", swap)
    contrib_own = jnp.einsum(
        "mtr,mtw->mrw", grads, hid_w[:, :, :col_width], preferred_element_type=jnp.float32
    ).astype(jnp.bfloat16)

    block_range = jnp.arange(blocks, dtype=jnp.int32)[None, :]
    selector = jnp.where(
        (live_flags[:, None] > 0) & (block_ids[:, None] == block_range), 1.0, 0.0
    ).astype(jnp.bfloat16)
    sel_by = selector.reshape(n_z, n_core, blocks)
    sel_own = lax.dynamic_index_in_dim(sel_by, core_at, 1, keepdims=False)
    sel_sib = lax.dynamic_index_in_dim(sel_by, 1 - core_at, 1, keepdims=False)
    n_own = contrib_own.shape[0]
    grad_head = jnp.dot(
        sel_own.T, contrib_own.reshape(n_own, -1), preferred_element_type=jnp.float32
    ) + jnp.dot(sel_sib.T, contrib_got.reshape(n_own, -1), preferred_element_type=jnp.float32)
    grad_head = grad_head.astype(jnp.bfloat16)
    ghid = lax.psum_scatter(ghid, "section", scatter_dimension=1, tiled=True)
    ghid, grad_head = lax.optimization_barrier((ghid, grad_head))
    grad_head = grad_head.reshape(blocks * block_rows, col_width)
    ghid = ghid.astype(jnp.bfloat16)
    ghid = lax.all_to_all(ghid[:, :, None], "z", split_axis=0, concat_axis=2, tiled=True)
    ghid = jnp.take(ghid.reshape(tok_local, n_z * n_core, col_width), pair_swap, axis=1)
    grad_hidden = ghid.reshape(1, tok_local, model_width)

    return (grad_hidden, grad_head)


def solution(mesh):
    n_section, n_dp = mesh.devices.shape
    chips = Mesh(mesh.devices.reshape(n_section, n_dp // 2, 2), ("section", "z", "core"))
    dp = ("z", "core")
    placed = (
        P(dp, "section", None),
        P("section", dp),
        P(None, "section"),
        P(None, "section"),
        P(dp, None, "section"),
    )
    return jax.shard_map(
        local,
        mesh=chips,
        in_specs=placed,
        out_specs=(P(dp, "section", None), P("section", dp)),
        check_vma=False,
    )
```

```python
import jax
import jax.numpy as jnp
from jax import lax
from jax.sharding import Mesh, PartitionSpec as P

neg_fill = -1e30


def local(hidden, head, block_id, block_live, teacher):
    z_at = lax.axis_index("z")
    core_at = lax.axis_index("core")
    n_z = lax.axis_size("z")
    n_core = lax.axis_size("core")
    my_replica = z_at * n_core + core_at
    tok_local = hidden.shape[1]
    model_width = hidden.shape[2]
    block_rows = teacher.shape[2]
    col_width = head.shape[1]
    blocks = head.shape[0] // block_rows
    table = head.reshape(blocks, block_rows, col_width)
    block_ids = block_id[:, 0]
    live_flags = block_live[:, 0]
    swap = [(0, 1), (1, 0)]

    ids_by = block_ids.reshape(n_z, n_core)
    own_ids = lax.dynamic_index_in_dim(ids_by, core_at, 1, keepdims=False)
    sib_ids = lax.dynamic_index_in_dim(ids_by, 1 - core_at, 1, keepdims=False)

    pair_swap = jnp.arange(n_z * n_core, dtype=jnp.int32) ^ core_at
    pieces = jnp.take(hidden[0].reshape(tok_local, n_z * n_core, col_width), pair_swap, axis=1)
    pieces = pieces.reshape(1, tok_local, n_z, n_core * col_width)
    pieces = lax.all_to_all(pieces, "z", split_axis=2, concat_axis=0, tiled=True)
    hid_w = lax.all_gather(pieces, "section", axis=1, tiled=True).reshape(n_z, -1, n_core * col_width)

    own_rows = jnp.take(table, own_ids, axis=0)
    sib_rows = lax.ppermute(jnp.take(table, sib_ids, axis=0), "core", swap)
    rows = jnp.concatenate([own_rows, sib_rows], axis=2)

    own_live = lax.dynamic_index_in_dim(live_flags, my_replica, 0, keepdims=False) > 0
    teach = teacher[0].astype(jnp.float32)
    live_value = jnp.where(own_live, 1.0, 0.0).astype(jnp.float32)

    def local_stats(values):
        top = jnp.where(own_live, jnp.max(values, axis=1), neg_fill)
        total = jnp.where(own_live, jnp.sum(jnp.exp(values - top[:, None]), axis=1), 0.0)
        return top, total

    def merged(tops, totals):
        top = jnp.max(tops, axis=0)
        return top, jnp.sum(totals * jnp.exp(tops - top[None, :]), axis=0)

    teach_top_s, teach_sum_s = local_stats(teach)
    live_row = jnp.broadcast_to(live_value, teach_top_s.shape)
    teach_all = lax.all_gather(jnp.stack([teach_top_s, teach_sum_s, live_row]), "section")
    teach_all, hid_w = lax.optimization_barrier((teach_all, hid_w))
    teach_top, teach_total = merged(teach_all[:, 0], teach_all[:, 1])
    live_count = jnp.sum(teach_all[:, 2, 0])

    part = jnp.einsum("mtw,mrw->mtr", hid_w, rows, preferred_element_type=jnp.float32)
    logits = lax.psum_scatter(part, "z", scatter_dimension=0, tiled=True)[0]

    stud_top_s, stud_sum_s = local_stats(logits)
    stud_all = lax.all_gather(jnp.stack([stud_top_s, stud_sum_s]), "section")
    stud_top, stud_total = merged(stud_all[:, 0], stud_all[:, 1])

    student = jnp.where(own_live, jnp.exp(logits - stud_top[:, None]) / stud_total[:, None], 0.0)
    teach_prob = jnp.where(
        own_live, jnp.exp(teach - teach_top[:, None]) / teach_total[:, None], 0.0
    )
    logit_grad = (block_rows * live_count * (student - teach_prob)).astype(jnp.bfloat16)
    grads = lax.all_gather(logit_grad[None], "z", axis=0, tiled=True)

    ghid = jnp.einsum("mtr,mrw->tmw", grads, rows, preferred_element_type=jnp.float32)
    ghid, grads = lax.optimization_barrier((ghid, grads))
    contrib_sib = jnp.einsum(
        "mtr,mtw->mrw", grads, hid_w[:, :, col_width:], preferred_element_type=jnp.float32
    ).astype(jnp.bfloat16)
    contrib_got = lax.ppermute(contrib_sib, "core", swap)
    contrib_own = jnp.einsum(
        "mtr,mtw->mrw", grads, hid_w[:, :, :col_width], preferred_element_type=jnp.float32
    ).astype(jnp.bfloat16)

    block_range = jnp.arange(blocks, dtype=jnp.int32)[None, :]
    selector = jnp.where(
        (live_flags[:, None] > 0) & (block_ids[:, None] == block_range), 1.0, 0.0
    ).astype(jnp.bfloat16)
    sel_by = selector.reshape(n_z, n_core, blocks)
    sel_own = lax.dynamic_index_in_dim(sel_by, core_at, 1, keepdims=False)
    sel_sib = lax.dynamic_index_in_dim(sel_by, 1 - core_at, 1, keepdims=False)
    n_own = contrib_own.shape[0]
    grad_head = jnp.dot(
        sel_own.T, contrib_own.reshape(n_own, -1), preferred_element_type=jnp.float32
    ) + jnp.dot(sel_sib.T, contrib_got.reshape(n_own, -1), preferred_element_type=jnp.float32)
    grad_head = grad_head.astype(jnp.bfloat16)
    ghid = lax.psum_scatter(ghid, "section", scatter_dimension=0, tiled=True)
    ghid, grad_head = lax.optimization_barrier((ghid, grad_head))
    grad_head = grad_head.reshape(blocks * block_rows, col_width)
    ghid = ghid.astype(jnp.bfloat16)
    ghid = lax.all_to_all(ghid, "z", split_axis=1, concat_axis=1, tiled=True)
    ghid = jnp.take(ghid.reshape(tok_local, n_z * n_core, col_width), pair_swap, axis=1)
    grad_hidden = ghid.reshape(1, tok_local, model_width)

    return (grad_hidden, grad_head)


def solution(mesh):
    n_section, n_dp = mesh.devices.shape
    chips = Mesh(mesh.devices.reshape(n_section, n_dp // 2, 2), ("section", "z", "core"))
    dp = ("z", "core")
    placed = (
        P(dp, "section", None),
        P("section", dp),
        P(None, "section"),
        P(None, "section"),
        P(dp, None, "section"),
    )
    return jax.shard_map(
        local,
        mesh=chips,
        in_specs=placed,
        out_specs=(P(dp, "section", None), P("section", dp)),
        check_vma=False,
    )
```

```python
import jax
import jax.numpy as jnp
from jax import lax
from jax.sharding import Mesh, PartitionSpec as P

neg_fill = -1e30


def local(hidden, head, block_id, block_live, teacher):
    z_at = lax.axis_index("z")
    core_at = lax.axis_index("core")
    n_z = lax.axis_size("z")
    n_core = lax.axis_size("core")
    my_replica = z_at * n_core + core_at
    tok_local = hidden.shape[1]
    model_width = hidden.shape[2]
    block_rows = teacher.shape[2]
    col_width = head.shape[1]
    blocks = head.shape[0] // block_rows
    table = head.reshape(blocks, block_rows, col_width)
    block_ids = block_id[:, 0]
    live_flags = block_live[:, 0]
    swap = [(0, 1), (1, 0)]

    ids_by = block_ids.reshape(n_z, n_core)
    own_ids = lax.dynamic_index_in_dim(ids_by, core_at, 1, keepdims=False)
    sib_ids = lax.dynamic_index_in_dim(ids_by, 1 - core_at, 1, keepdims=False)

    pair_swap = jnp.arange(n_z * n_core, dtype=jnp.int32) ^ core_at
    pieces = jnp.take(hidden[0].reshape(tok_local, n_z * n_core, col_width), pair_swap, axis=1)
    pieces = pieces.reshape(1, tok_local, n_z, n_core * col_width)
    pieces = lax.all_to_all(pieces, "z", split_axis=2, concat_axis=0, tiled=True)
    hid_w = lax.all_gather(pieces, "section", axis=1, tiled=True).reshape(n_z, -1, n_core * col_width)

    own_rows = jnp.take(table, own_ids, axis=0)
    sib_rows = lax.ppermute(jnp.take(table, sib_ids, axis=0), "core", swap)
    rows = jnp.concatenate([own_rows, sib_rows], axis=2)

    own_live = lax.dynamic_index_in_dim(live_flags, my_replica, 0, keepdims=False) > 0
    teach = teacher[0].astype(jnp.float32)
    live_value = jnp.where(own_live, 1.0, 0.0).astype(jnp.float32)

    def local_stats(values):
        top = jnp.where(own_live, jnp.max(values, axis=1), neg_fill)
        total = jnp.where(own_live, jnp.sum(jnp.exp(values - top[:, None]), axis=1), 0.0)
        return top, total

    def merged(tops, totals):
        top = jnp.max(tops, axis=0)
        return top, jnp.sum(totals * jnp.exp(tops - top[None, :]), axis=0)

    teach_top_s, teach_sum_s = local_stats(teach)
    live_row = jnp.broadcast_to(live_value, teach_top_s.shape)
    teach_all = lax.all_gather(jnp.stack([teach_top_s, teach_sum_s, live_row]), "section")
    teach_all, hid_w = lax.optimization_barrier((teach_all, hid_w))
    teach_top, teach_total = merged(teach_all[:, 0], teach_all[:, 1])
    live_count = jnp.sum(teach_all[:, 2, 0])
    teach_prob = jnp.where(
        own_live, jnp.exp(teach - teach_top[:, None]) / teach_total[:, None], 0.0
    )
    teach_prob = lax.optimization_barrier(teach_prob)

    part = jnp.einsum("mtw,mrw->mtr", hid_w, rows, preferred_element_type=jnp.float32)
    logits = lax.psum_scatter(part, "z", scatter_dimension=0, tiled=True)[0]

    stud_top_s, stud_sum_s = local_stats(logits)
    stud_all = lax.all_gather(jnp.stack([stud_top_s, stud_sum_s]), "section")
    stud_top, stud_total = merged(stud_all[:, 0], stud_all[:, 1])

    student = jnp.where(own_live, jnp.exp(logits - stud_top[:, None]) / stud_total[:, None], 0.0)
    logit_grad = (block_rows * live_count * (student - teach_prob)).astype(jnp.bfloat16)
    grads = lax.all_gather(logit_grad[None], "z", axis=0, tiled=True)

    ghid = jnp.einsum("mtr,mrw->mtw", grads, rows, preferred_element_type=jnp.float32)
    ghid, grads = lax.optimization_barrier((ghid, grads))
    contrib_sib = jnp.einsum(
        "mtr,mtw->mrw", grads, hid_w[:, :, col_width:], preferred_element_type=jnp.float32
    ).astype(jnp.bfloat16)
    contrib_got = lax.ppermute(contrib_sib, "core", swap)
    contrib_own = jnp.einsum(
        "mtr,mtw->mrw", grads, hid_w[:, :, :col_width], preferred_element_type=jnp.float32
    ).astype(jnp.bfloat16)

    block_range = jnp.arange(blocks, dtype=jnp.int32)[None, :]
    selector = jnp.where(
        (live_flags[:, None] > 0) & (block_ids[:, None] == block_range), 1.0, 0.0
    ).astype(jnp.bfloat16)
    sel_by = selector.reshape(n_z, n_core, blocks)
    sel_own = lax.dynamic_index_in_dim(sel_by, core_at, 1, keepdims=False)
    sel_sib = lax.dynamic_index_in_dim(sel_by, 1 - core_at, 1, keepdims=False)
    n_own = contrib_own.shape[0]
    grad_head = jnp.dot(
        sel_own.T, contrib_own.reshape(n_own, -1), preferred_element_type=jnp.float32
    ) + jnp.dot(sel_sib.T, contrib_got.reshape(n_own, -1), preferred_element_type=jnp.float32)
    grad_head = grad_head.astype(jnp.bfloat16)
    ghid = lax.psum_scatter(ghid, "section", scatter_dimension=1, tiled=True)
    ghid, grad_head = lax.optimization_barrier((ghid, grad_head))
    grad_head = grad_head.reshape(blocks * block_rows, col_width)
    ghid = ghid.astype(jnp.bfloat16)
    ghid = lax.all_to_all(ghid[:, :, None], "z", split_axis=0, concat_axis=2, tiled=True)
    ghid = jnp.take(ghid.reshape(tok_local, n_z * n_core, col_width), pair_swap, axis=1)
    grad_hidden = ghid.reshape(1, tok_local, model_width)

    return (grad_hidden, grad_head)


def solution(mesh):
    n_section, n_dp = mesh.devices.shape
    chips = Mesh(mesh.devices.reshape(n_section, n_dp // 2, 2), ("section", "z", "core"))
    dp = ("z", "core")
    placed = (
        P(dp, "section", None),
        P("section", dp),
        P(None, "section"),
        P(None, "section"),
        P(dp, None, "section"),
    )
    return jax.shard_map(
        local,
        mesh=chips,
        in_specs=placed,
        out_specs=(P(dp, "section", None), P("section", dp)),
        check_vma=False,
    )
```

```python
import jax
import jax.numpy as jnp
from jax import lax
from jax.sharding import Mesh, PartitionSpec as P

neg_fill = -1e30


def local(hidden, head, block_id, block_live, teacher):
    z_at = lax.axis_index("z")
    core_at = lax.axis_index("core")
    n_z = lax.axis_size("z")
    n_core = lax.axis_size("core")
    my_replica = z_at * n_core + core_at
    tok_local = hidden.shape[1]
    model_width = hidden.shape[2]
    block_rows = teacher.shape[2]
    col_width = head.shape[1]
    blocks = head.shape[0] // block_rows
    table = head.reshape(blocks, block_rows, col_width)
    block_ids = block_id[:, 0]
    live_flags = block_live[:, 0]
    swap = [(0, 1), (1, 0)]

    ids_by = block_ids.reshape(n_z, n_core)
    own_ids = lax.dynamic_index_in_dim(ids_by, core_at, 1, keepdims=False)
    sib_ids = lax.dynamic_index_in_dim(ids_by, 1 - core_at, 1, keepdims=False)

    pair_swap = jnp.arange(n_z * n_core, dtype=jnp.int32) ^ core_at
    pieces = jnp.take(hidden[0].reshape(tok_local, n_z * n_core, col_width), pair_swap, axis=1)
    pieces = pieces.reshape(1, tok_local, n_z, n_core * col_width)
    pieces = lax.all_to_all(pieces, "z", split_axis=2, concat_axis=0, tiled=True)
    hid_w = lax.all_gather(pieces, "section", axis=1, tiled=True).reshape(n_z, -1, n_core * col_width)

    own_rows = jnp.take(table, own_ids, axis=0)
    sib_rows = lax.ppermute(jnp.take(table, sib_ids, axis=0), "core", swap)
    rows = jnp.concatenate([own_rows, sib_rows], axis=2)

    own_live = lax.dynamic_index_in_dim(live_flags, my_replica, 0, keepdims=False) > 0
    teach = teacher[0].astype(jnp.float32)
    live_value = jnp.where(own_live, 1.0, 0.0).astype(jnp.float32)

    dead_shift = jnp.where(own_live, 0.0, neg_fill).astype(jnp.float32)

    def local_stats(values):
        top = jnp.max(values, axis=1)
        total = live_value * jnp.sum(jnp.exp(values - top[:, None]), axis=1)
        return top + dead_shift, total

    def merged(tops, totals):
        top = jnp.max(tops, axis=0)
        return top, jnp.sum(totals * jnp.exp(tops - top[None, :]), axis=0)

    teach_top_s, teach_sum_s = local_stats(teach)
    live_row = jnp.broadcast_to(live_value, teach_top_s.shape)
    teach_all = lax.all_gather(jnp.stack([teach_top_s, teach_sum_s, live_row]), "section")
    teach_all, hid_w = lax.optimization_barrier((teach_all, hid_w))
    teach_top, teach_total = merged(teach_all[:, 0], teach_all[:, 1])
    live_count = jnp.sum(teach_all[:, 2, 0])

    part = jnp.einsum("mtw,mrw->mtr", hid_w, rows, preferred_element_type=jnp.float32)
    logits = lax.psum_scatter(part, "z", scatter_dimension=0, tiled=True)[0]

    stud_top_s, stud_sum_s = local_stats(logits)
    stud_all = lax.all_gather(jnp.stack([stud_top_s, stud_sum_s]), "section")
    stud_top, stud_total = merged(stud_all[:, 0], stud_all[:, 1])

    student = jnp.where(own_live, jnp.exp(logits - stud_top[:, None]) / stud_total[:, None], 0.0)
    teach_prob = jnp.where(
        own_live, jnp.exp(teach - teach_top[:, None]) / teach_total[:, None], 0.0
    )
    logit_grad = (block_rows * live_count * (student - teach_prob)).astype(jnp.bfloat16)
    grads = lax.all_gather(logit_grad[None], "z", axis=0, tiled=True)

    ghid = jnp.einsum("mtr,mrw->mtw", grads, rows, preferred_element_type=jnp.float32)
    ghid, grads = lax.optimization_barrier((ghid, grads))
    contrib_sib = jnp.einsum(
        "mtr,mtw->mrw", grads, hid_w[:, :, col_width:], preferred_element_type=jnp.float32
    ).astype(jnp.bfloat16)
    contrib_got = lax.ppermute(contrib_sib, "core", swap)
    contrib_own = jnp.einsum(
        "mtr,mtw->mrw", grads, hid_w[:, :, :col_width], preferred_element_type=jnp.float32
    ).astype(jnp.bfloat16)

    block_range = jnp.arange(blocks, dtype=jnp.int32)[None, :]
    selector = jnp.where(
        (live_flags[:, None] > 0) & (block_ids[:, None] == block_range), 1.0, 0.0
    ).astype(jnp.bfloat16)
    sel_by = selector.reshape(n_z, n_core, blocks)
    sel_own = lax.dynamic_index_in_dim(sel_by, core_at, 1, keepdims=False)
    sel_sib = lax.dynamic_index_in_dim(sel_by, 1 - core_at, 1, keepdims=False)
    n_own = contrib_own.shape[0]
    grad_head = jnp.dot(
        sel_own.T, contrib_own.reshape(n_own, -1), preferred_element_type=jnp.float32
    ) + jnp.dot(sel_sib.T, contrib_got.reshape(n_own, -1), preferred_element_type=jnp.float32)
    grad_head = grad_head.astype(jnp.bfloat16)
    ghid = lax.psum_scatter(ghid, "section", scatter_dimension=1, tiled=True)
    ghid, grad_head = lax.optimization_barrier((ghid, grad_head))
    grad_head = grad_head.reshape(blocks * block_rows, col_width)
    ghid = lax.all_to_all(ghid[:, :, None], "z", split_axis=0, concat_axis=2, tiled=True)
    ghid = jnp.take(ghid.reshape(tok_local, n_z * n_core, col_width), pair_swap, axis=1)
    grad_hidden = ghid.astype(jnp.bfloat16).reshape(1, tok_local, model_width)

    return (grad_hidden, grad_head)


def solution(mesh):
    n_section, n_dp = mesh.devices.shape
    chips = Mesh(mesh.devices.reshape(n_section, n_dp // 2, 2), ("section", "z", "core"))
    dp = ("z", "core")
    placed = (
        P(dp, "section", None),
        P("section", dp),
        P(None, "section"),
        P(None, "section"),
        P(dp, None, "section"),
    )
    return jax.shard_map(
        local,
        mesh=chips,
        in_specs=placed,
        out_specs=(P(dp, "section", None), P("section", dp)),
        check_vma=False,
    )
```

```python
import jax
import jax.numpy as jnp
from jax import lax
from jax.sharding import Mesh, PartitionSpec as P

neg_fill = -1e30


def local(hidden, head, block_id, block_live, teacher):
    z_at = lax.axis_index("z")
    core_at = lax.axis_index("core")
    n_z = lax.axis_size("z")
    n_core = lax.axis_size("core")
    my_replica = z_at * n_core + core_at
    tok_local = hidden.shape[1]
    model_width = hidden.shape[2]
    block_rows = teacher.shape[2]
    col_width = head.shape[1]
    blocks = head.shape[0] // block_rows
    table = head.reshape(blocks, block_rows, col_width)
    block_ids = block_id[:, 0]
    live_flags = block_live[:, 0]
    swap = [(0, 1), (1, 0)]

    ids_by = block_ids.reshape(n_z, n_core)
    own_ids = lax.dynamic_index_in_dim(ids_by, core_at, 1, keepdims=False)
    sib_ids = lax.dynamic_index_in_dim(ids_by, 1 - core_at, 1, keepdims=False)

    pair_swap = jnp.arange(n_z * n_core, dtype=jnp.int32) ^ core_at
    pieces = jnp.take(hidden[0].reshape(tok_local, n_z * n_core, col_width), pair_swap, axis=1)
    pieces = pieces.reshape(1, tok_local, n_z, n_core * col_width)
    pieces = lax.all_to_all(pieces, "z", split_axis=2, concat_axis=0, tiled=True)
    hid_w = lax.all_gather(pieces, "section", axis=1, tiled=True).reshape(n_z, -1, n_core * col_width)

    own_rows = jnp.take(table, own_ids, axis=0)
    sib_rows = lax.ppermute(jnp.take(table, sib_ids, axis=0), "core", swap)
    rows = jnp.concatenate([own_rows, sib_rows], axis=2)
    odd = core_at == 1
    rows_natural = jnp.concatenate(
        [jnp.where(odd, sib_rows, own_rows), jnp.where(odd, own_rows, sib_rows)], axis=2
    )

    own_live = lax.dynamic_index_in_dim(live_flags, my_replica, 0, keepdims=False) > 0
    teach = teacher[0].astype(jnp.float32)
    live_value = jnp.where(own_live, 1.0, 0.0).astype(jnp.float32)

    dead_shift = jnp.where(own_live, 0.0, neg_fill).astype(jnp.float32)

    def local_stats(values):
        top = jnp.max(values, axis=1)
        total = live_value * jnp.sum(jnp.exp(values - top[:, None]), axis=1)
        return top + dead_shift, total

    def merged(tops, totals):
        top = jnp.max(tops, axis=0)
        return top, jnp.sum(totals * jnp.exp(tops - top[None, :]), axis=0)

    teach_top_s, teach_sum_s = local_stats(teach)
    live_row = jnp.broadcast_to(live_value, teach_top_s.shape)
    teach_all = lax.all_gather(jnp.stack([teach_top_s, teach_sum_s, live_row]), "section")
    teach_all, hid_w = lax.optimization_barrier((teach_all, hid_w))
    teach_top, teach_total = merged(teach_all[:, 0], teach_all[:, 1])
    live_count = jnp.sum(teach_all[:, 2, 0])

    part = jnp.einsum("mtw,mrw->mtr", hid_w, rows, preferred_element_type=jnp.float32)
    logits = lax.psum_scatter(part, "z", scatter_dimension=0, tiled=True)[0]

    stud_top_s, stud_sum_s = local_stats(logits)
    stud_all = lax.all_gather(jnp.stack([stud_top_s, stud_sum_s]), "section")
    stud_top, stud_total = merged(stud_all[:, 0], stud_all[:, 1])

    student = jnp.where(own_live, jnp.exp(logits - stud_top[:, None]) / stud_total[:, None], 0.0)
    teach_prob = jnp.where(
        own_live, jnp.exp(teach - teach_top[:, None]) / teach_total[:, None], 0.0
    )
    logit_grad = (block_rows * live_count * (student - teach_prob)).astype(jnp.bfloat16)
    grads = lax.all_gather(logit_grad[None], "z", axis=0, tiled=True)

    ghid = jnp.einsum("mtr,mrw->mtw", grads, rows_natural, preferred_element_type=jnp.float32)
    ghid, grads = lax.optimization_barrier((ghid, grads))
    contrib_sib = jnp.einsum(
        "mtr,mtw->mrw", grads, hid_w[:, :, col_width:], preferred_element_type=jnp.float32
    ).astype(jnp.bfloat16)
    contrib_got = lax.ppermute(contrib_sib, "core", swap)
    contrib_own = jnp.einsum(
        "mtr,mtw->mrw", grads, hid_w[:, :, :col_width], preferred_element_type=jnp.float32
    ).astype(jnp.bfloat16)

    block_range = jnp.arange(blocks, dtype=jnp.int32)[None, :]
    selector = jnp.where(
        (live_flags[:, None] > 0) & (block_ids[:, None] == block_range), 1.0, 0.0
    ).astype(jnp.bfloat16)
    sel_by = selector.reshape(n_z, n_core, blocks)
    sel_own = lax.dynamic_index_in_dim(sel_by, core_at, 1, keepdims=False)
    sel_sib = lax.dynamic_index_in_dim(sel_by, 1 - core_at, 1, keepdims=False)
    n_own = contrib_own.shape[0]
    grad_head = jnp.dot(
        sel_own.T, contrib_own.reshape(n_own, -1), preferred_element_type=jnp.float32
    ) + jnp.dot(sel_sib.T, contrib_got.reshape(n_own, -1), preferred_element_type=jnp.float32)
    grad_head = grad_head.astype(jnp.bfloat16)
    ghid = lax.psum_scatter(ghid, "section", scatter_dimension=1, tiled=True)
    ghid, grad_head = lax.optimization_barrier((ghid, grad_head))
    grad_head = grad_head.reshape(blocks * block_rows, col_width)
    ghid = lax.all_to_all(ghid[:, :, None], "z", split_axis=0, concat_axis=2, tiled=True)
    grad_hidden = ghid.astype(jnp.bfloat16).reshape(1, tok_local, model_width)

    return (grad_hidden, grad_head)


def solution(mesh):
    n_section, n_dp = mesh.devices.shape
    chips = Mesh(mesh.devices.reshape(n_section, n_dp // 2, 2), ("section", "z", "core"))
    dp = ("z", "core")
    placed = (
        P(dp, "section", None),
        P("section", dp),
        P(None, "section"),
        P(None, "section"),
        P(dp, None, "section"),
    )
    return jax.shard_map(
        local,
        mesh=chips,
        in_specs=placed,
        out_specs=(P(dp, "section", None), P("section", dp)),
        check_vma=False,
    )
```

```python
import jax
import jax.numpy as jnp
from jax import lax
from jax.sharding import Mesh, PartitionSpec as P

neg_fill = -1e30


def local(hidden, head, block_id, block_live, teacher):
    z_at = lax.axis_index("z")
    core_at = lax.axis_index("core")
    n_z = lax.axis_size("z")
    n_core = lax.axis_size("core")
    my_replica = z_at * n_core + core_at
    tok_local = hidden.shape[1]
    model_width = hidden.shape[2]
    block_rows = teacher.shape[2]
    col_width = head.shape[1]
    blocks = head.shape[0] // block_rows
    table = head.reshape(blocks, block_rows, col_width)
    block_ids = block_id[:, 0]
    live_flags = block_live[:, 0]
    swap = [(0, 1), (1, 0)]

    ids_by = block_ids.reshape(n_z, n_core)
    own_ids = lax.dynamic_index_in_dim(ids_by, core_at, 1, keepdims=False)
    sib_ids = lax.dynamic_index_in_dim(ids_by, 1 - core_at, 1, keepdims=False)

    pieces = hidden.reshape(1, tok_local, n_z, n_core * col_width)
    pieces = lax.all_to_all(pieces, "z", split_axis=2, concat_axis=0, tiled=True)
    hid_w = lax.all_gather(pieces, "section", axis=1, tiled=True).reshape(n_z, -1, n_core * col_width)

    own_rows = jnp.take(table, own_ids, axis=0)
    sib_rows = lax.ppermute(jnp.take(table, sib_ids, axis=0), "core", swap)
    odd = core_at == 1
    rows_natural = jnp.concatenate(
        [jnp.where(odd, sib_rows, own_rows), jnp.where(odd, own_rows, sib_rows)], axis=2
    )

    own_live = lax.dynamic_index_in_dim(live_flags, my_replica, 0, keepdims=False) > 0
    teach = teacher[0].astype(jnp.float32)
    live_value = jnp.where(own_live, 1.0, 0.0).astype(jnp.float32)

    dead_shift = jnp.where(own_live, 0.0, neg_fill).astype(jnp.float32)

    def local_stats(values):
        top = jnp.max(values, axis=1)
        total = live_value * jnp.sum(jnp.exp(values - top[:, None]), axis=1)
        return top + dead_shift, total

    def merged(tops, totals):
        top = jnp.max(tops, axis=0)
        return top, jnp.sum(totals * jnp.exp(tops - top[None, :]), axis=0)

    teach_top_s, teach_sum_s = local_stats(teach)
    live_row = jnp.broadcast_to(live_value, teach_top_s.shape)
    teach_all = lax.all_gather(jnp.stack([teach_top_s, teach_sum_s, live_row]), "section")
    teach_all, hid_w = lax.optimization_barrier((teach_all, hid_w))
    teach_top, teach_total = merged(teach_all[:, 0], teach_all[:, 1])
    live_count = jnp.sum(teach_all[:, 2, 0])

    part = jnp.einsum("mtw,mrw->mtr", hid_w, rows_natural, preferred_element_type=jnp.float32)
    logits = lax.psum_scatter(part, "z", scatter_dimension=0, tiled=True)[0]

    stud_top_s, stud_sum_s = local_stats(logits)
    stud_all = lax.all_gather(jnp.stack([stud_top_s, stud_sum_s]), "section")
    stud_top, stud_total = merged(stud_all[:, 0], stud_all[:, 1])

    student = jnp.where(own_live, jnp.exp(logits - stud_top[:, None]) / stud_total[:, None], 0.0)
    teach_prob = jnp.where(
        own_live, jnp.exp(teach - teach_top[:, None]) / teach_total[:, None], 0.0
    )
    logit_grad = (block_rows * live_count * (student - teach_prob)).astype(jnp.bfloat16)
    grads = lax.all_gather(logit_grad[None], "z", axis=0, tiled=True)

    ghid = jnp.einsum("mtr,mrw->mtw", grads, rows_natural, preferred_element_type=jnp.float32)
    ghid, grads = lax.optimization_barrier((ghid, grads))
    contrib_sib = jnp.einsum(
        "mtr,mtw->mrw", grads, lax.dynamic_slice_in_dim(hid_w, (1 - core_at) * col_width, col_width, 2), preferred_element_type=jnp.float32
    ).astype(jnp.bfloat16)
    contrib_got = lax.ppermute(contrib_sib, "core", swap)
    contrib_own = jnp.einsum(
        "mtr,mtw->mrw", grads, lax.dynamic_slice_in_dim(hid_w, core_at * col_width, col_width, 2), preferred_element_type=jnp.float32
    ).astype(jnp.bfloat16)

    block_range = jnp.arange(blocks, dtype=jnp.int32)[None, :]
    selector = jnp.where(
        (live_flags[:, None] > 0) & (block_ids[:, None] == block_range), 1.0, 0.0
    ).astype(jnp.bfloat16)
    sel_by = selector.reshape(n_z, n_core, blocks)
    sel_own = lax.dynamic_index_in_dim(sel_by, core_at, 1, keepdims=False)
    sel_sib = lax.dynamic_index_in_dim(sel_by, 1 - core_at, 1, keepdims=False)
    n_own = contrib_own.shape[0]
    grad_head = jnp.dot(
        sel_own.T, contrib_own.reshape(n_own, -1), preferred_element_type=jnp.float32
    ) + jnp.dot(sel_sib.T, contrib_got.reshape(n_own, -1), preferred_element_type=jnp.float32)
    grad_head = grad_head.astype(jnp.bfloat16)
    ghid = lax.psum_scatter(ghid, "section", scatter_dimension=1, tiled=True)
    ghid, grad_head = lax.optimization_barrier((ghid, grad_head))
    grad_head = grad_head.reshape(blocks * block_rows, col_width)
    ghid = lax.all_to_all(ghid[:, :, None], "z", split_axis=0, concat_axis=2, tiled=True)
    grad_hidden = ghid.astype(jnp.bfloat16).reshape(1, tok_local, model_width)

    return (grad_hidden, grad_head)


def solution(mesh):
    n_section, n_dp = mesh.devices.shape
    chips = Mesh(mesh.devices.reshape(n_section, n_dp // 2, 2), ("section", "z", "core"))
    dp = ("z", "core")
    placed = (
        P(dp, "section", None),
        P("section", dp),
        P(None, "section"),
        P(None, "section"),
        P(dp, None, "section"),
    )
    return jax.shard_map(
        local,
        mesh=chips,
        in_specs=placed,
        out_specs=(P(dp, "section", None), P("section", dp)),
        check_vma=False,
    )
```
